256 devices in a mesh: seq: 16 (over x, y), exp: 16 (over z, core).
Axes of the slice: x: 4, y: 4, z: 8, core: 2. Of those that a mesh axis runs over, the one named last changes fastest.
Arguments:
- mixer_input: bfloat16 [16384, 4096], P('seq', 'exp'), may hold values from -6 to 6
- gate_input: bfloat16 [16384, 4096], P('seq', 'exp'), may hold values from -6 to 6
- write_keys: bfloat16 [16384, 128], P('seq'), may hold values from -6 to 6
- read_queries: bfloat16 [16384, 128], P('seq'), may hold values from -0.5 to 0.5
- step_size: float32 [64, 16384], P('exp', 'seq'), may hold values from 0 to 1, as said below
- log_decay: float32 [64, 16384], P('exp', 'seq'), may hold values from -1 to 0, as said below
- skip_gain: float32 [64], P('exp'), may hold values from 0.5 to 1.5
- out_weight: bfloat16 [4096, 2048], P('exp'), may hold values from -0.09375 to 0.09375
- residual: bfloat16 [16384, 2048], P(('seq', 'exp')), may hold values from -6 to 6
- norm_gain: float32 [2048], replicated, may hold values from 0.25 to 1.75
- routes: int32 [16384, 6], P(('seq', 'exp')), may hold values from 0 to 63, all different within a row; in each aligned block of 64 rows (0 to 63, 64 to 127, ...) at most 8 rows name the same one
- route_weight: float32 [16384, 6], P(('seq', 'exp')), may hold values from 0.1 to 0.5
- expert_gate: bfloat16 [256, 352, 2048], P(('seq', 'exp')), may hold values from -0.125 to 0.125
- expert_up: bfloat16 [256, 352, 2048], P(('seq', 'exp')), may hold values from -0.125 to 0.125
- expert_down: bfloat16 [256, 352, 2048], P(('seq', 'exp')), may hold values from -0.15625 to 0.15625
Outputs:
- block_output: bfloat16 [16384, 2048], P(('seq', 'exp'))
The draws below stay inside these ranges and needn't reach their ends.
Inputs may be any that keep to these rules, and one draw needn't show every extreme that they name: `routes`: each row names 6 different experts; in each aligned block of 64 rows (the rows of one device) no expert is named by more than 8 rows, a bound that some block reaches. `step_size`: positive. `log_decay`: not positive.
All inputs are finite; a program needn't handle non-finite values.
Results may differ from the reference program's by a relative error of at most 0.015.
Values may be sent and summed in bfloat16 or wider, within the bound.
No kernel may reach another device: no remote copies, remote signals or barrier semaphores. Data moves between devices by JAX's collectives and lax.ppermute only.
A program may use at most 128 MiB of HBM per device.

```python
import math
import jax
import jax.numpy as jnp
import numpy as np
from jax import lax

D = 2048
HEADS = 64
HEAD_DIM = 64
STATE = 128
FF = 1408
TOP = 6
SPLIT = 4
STRETCH = 256
INNER = 4096
TOKENS = 16384
ROWS = 64
EXPERTS = 64
PIECE = 352
CAP = 8
N_EXP = 16


def decay_plan(key):
    base = jax.random.fold_in(key, 11)
    key_slow, key_rate, key_fast = jax.random.split(base, 3)
    slow_share = 0.6
    slow_heads = jax.random.uniform(key_slow, (HEADS,)) < slow_share
    rate_slow = jnp.exp(jax.random.uniform(key_rate, (HEADS,), minval=math.log(0.05 / TOKENS), maxval=math.log(0.5 / TOKENS)))
    rate_fast = jnp.exp(jax.random.uniform(key_fast, (HEADS,), minval=math.log(1.0 / 50.0), maxval=math.log(1.0 / 30.0)))
    decay_speeds = jnp.where(slow_heads, rate_slow, rate_fast)
    levels = jnp.where(slow_heads, 0.7 / math.sqrt(TOKENS), 0.11)
    return (decay_speeds, levels)


def draw_log_decay(key, part):
    decay_speeds, levels = decay_plan(key)
    key_block, key_rough, key_place, key_amount = jax.random.split(jax.random.fold_in(key, 23), 4)
    blocks = TOKENS // STRETCH
    block_multiplier = jnp.exp(jax.random.uniform(key_block, (HEADS, blocks), minval=math.log(0.3), maxval=math.log(3.0)))
    block_multiplier = jnp.repeat(block_multiplier, STRETCH, axis=1)
    jitter_level = jax.random.uniform(key_rough, (HEADS, TOKENS), minval=0.5, maxval=1.5)
    token_offsets = jax.random.randint(key_place, (3,), 0, TOKENS)
    load_amount_values = -jnp.log(1.0 - jax.random.uniform(key_amount, (3,), minval=0.2, maxval=0.35))
    location_values = jnp.arange(TOKENS)
    spike_events = jnp.sum(jnp.where(location_values[None, :] == token_offsets[:, None], load_amount_values[:, None], 0.0), axis=0)
    return (-(decay_speeds[:, None] * block_multiplier * jitter_level) - spike_events[None, :]).astype(jnp.float32)


def draw_step_size(key, part):
    decay_speeds, levels = decay_plan(key)
    key_rough = jax.random.fold_in(key, 31)
    jitter_level = jax.random.uniform(key_rough, (HEADS, TOKENS), minval=0.5, maxval=1.5)
    return (levels[:, None] * jitter_level).astype(jnp.float32)


def steps_of(own_key, shape, cuts, low, largest):
    def one(axis_at, blocks):
        heights = jax.random.uniform(jax.random.fold_in(jax.random.fold_in(own_key, 6), axis_at), (blocks,), jnp.float32, low / len(cuts), largest / len(cuts))
        return jnp.repeat(jnp.exp(heights), shape[axis_at] // blocks).reshape((-1,) + (1,) * (len(shape) - axis_at - 1))

    factor_of = one(*cuts[0])
    for cut in cuts[1:]:
        factor_of = factor_of * one(*cut)
    return factor_of


def assign_block(stream_key, own, number, rows, count, top, most, skew):
    order = jax.random.permutation(stream_key, count)
    heavy_load, ordinary = load_shares(count, rows * top, most, skew, True), load_shares(count, rows * top, most, skew, False)
    places = jnp.arange(count)

    def named(lengths, offset_by):
        used = int((lengths > 0).sum())
        fixed = max(1, used // 4)
        passed = fixed + (places - fixed + offset_by * (used - fixed)) % max(1, count - fixed)
        return jnp.zeros((count,), jnp.int32).at[order[jnp.where(places < fixed, places, passed)]].set(jnp.asarray(lengths, jnp.int32))

    lengths = jnp.where(number % 4 == 0, named(heavy_load, number // 4), named(ordinary, number - number // 4 - 1))
    mixed = jax.random.permutation(jax.random.fold_in(own, 3), count)
    donor, taker = mixed[0:count // 2 * 2:2], mixed[1:count // 2 * 2:2]
    slack = jnp.minimum(lengths[donor] - 1, most - lengths[taker]) // 2
    slack = jnp.where((donor == order[0]) | (taker == order[0]) | (lengths[taker] == 0), 0, jnp.maximum(slack, 0))
    passed = jax.random.randint(jax.random.fold_in(own, 4), (count // 2,), 0, 1 << 20) % (slack + 1)
    lengths = lengths.at[donor].add(-passed).at[taker].add(passed)
    labels = jnp.searchsorted(jnp.cumsum(lengths), jnp.arange(rows * top), side="right").astype(jnp.int32)
    grid = labels.reshape(top, rows).T
    grid = grid[jax.random.permutation(jax.random.fold_in(own, 1), rows)]
    offset_by = jax.random.randint(jax.random.fold_in(own, 2), (rows, 1), 0, top)
    return jnp.take_along_axis(grid, (jnp.arange(top)[None, :] + offset_by) % top, axis=1)


def load_shares(count, total, bound, lean, full):
    loads = [(1 << 20) // math.isqrt(standing ** lean) + 1 for standing in range(1, count + 1)]
    largest = bound if full else min(bound, max(-(-total // count), total * loads[0] // sum(loads)))
    least = 1 if total - largest >= count - 1 else 0
    given, surplus = [largest] + [least] * (count - 1), total - largest - least * (count - 1)
    while surplus > 0:
        free = [i for i in range(1, count) if given[i] < largest] or [i for i in range(1, count) if given[i] < bound]
        mass, remaining = sum([loads[i] for i in free]), surplus
        for i in free:
            more = min(bound - given[i], max(1, remaining * loads[i] // mass), surplus)
            given[i] = given[i] + more
            surplus = surplus - more
    return np.array(given)


def noise(stream_key, dims, deviation, reach, cuts=(), kind=jnp.bfloat16):
    drawn = deviation * jax.random.normal(stream_key, dims, jnp.float32)
    if cuts:
        drawn = drawn * steps_of(stream_key, dims, cuts, -0.22, 0.18)
    return jnp.clip(drawn, -reach, reach).astype(kind)


def setup_inputs(seed: int = 0) -> dict:
    key_of = jax.random.split(jax.random.key(seed), 16)
    mixer_input = noise(key_of[0], (TOKENS, INNER), 1.0, 6.0, ((0, 16), (1, 16)))
    gate_input = noise(key_of[1], (TOKENS, INNER), 1.0, 6.0, ((0, 16), (1, 16)))
    write_keys = noise(key_of[2], (TOKENS, STATE), 1.0, 6.0, ((0, 16),))
    read_queries = noise(key_of[3], (TOKENS, STATE), STATE ** -0.5, 0.5, ((0, 16),))
    step_size = draw_step_size(jax.random.fold_in(key_of[15], 71), 0)
    log_decay = draw_log_decay(jax.random.fold_in(key_of[15], 71), 0)
    skip_gain = jnp.clip(0.5 + 1.0 * jax.random.uniform(key_of[6], (HEADS,), jnp.float32) ** steps_of(key_of[6], (HEADS,), ((0, 16),), -0.2, 0.2), 0.5, 1.5)
    out_weight = noise(key_of[7], (INNER, D), INNER ** -0.5, 0.09375, ((0, 16),))
    residual = noise(key_of[8], (TOKENS, D), 1.0, 6.0, ((0, 256),))
    norm_gain = jnp.clip(1.0 + 0.15 * jax.random.normal(key_of[9], (D,), jnp.float32), 0.25, 1.75)
    routes_keys = jax.random.split(jax.random.fold_in(key_of[10], 1), TOKENS // ROWS)
    routes_turns = jax.random.permutation(jax.random.fold_in(key_of[10], 3), TOKENS // ROWS)
    routes = jax.vmap(lambda own, number: assign_block(jax.random.fold_in(key_of[10], 2), own, number, ROWS, EXPERTS, TOP, CAP, 2))(routes_keys, routes_turns).reshape((TOKENS, TOP))
    route_weight = jnp.clip(0.1 + 0.4 * jax.random.uniform(key_of[11], (TOKENS, TOP), jnp.float32) ** steps_of(key_of[11], (TOKENS, TOP), ((0, 256),), -0.2, 0.2), 0.1, 0.5)
    expert_gate = noise(key_of[12], (EXPERTS * SPLIT, PIECE, D), D ** -0.5, 0.125, ((0, 256),))
    expert_up = noise(key_of[13], (EXPERTS * SPLIT, PIECE, D), D ** -0.5, 0.125, ((0, 256),))
    expert_down = noise(key_of[14], (EXPERTS * SPLIT, PIECE, D), FF ** -0.5, 0.15625, ((0, 256),))
    return dict(mixer_input=mixer_input, gate_input=gate_input, write_keys=write_keys, read_queries=read_queries, step_size=step_size, log_decay=log_decay, skip_gain=skip_gain, out_weight=out_weight, residual=residual, norm_gain=norm_gain, routes=routes, route_weight=route_weight, expert_gate=expert_gate, expert_up=expert_up, expert_down=expert_down)


def mixer_blocks(mixer_input, write_keys, read_queries, step_size, log_decay, skip_gain):
    blocks = TOKENS // STRETCH
    inputs = mixer_input.reshape(blocks, STRETCH, HEADS, HEAD_DIM)
    key_rows = write_keys.reshape(blocks, STRETCH, STATE)
    queries = read_queries.reshape(blocks, STRETCH, STATE)
    step_rows = step_size.reshape(HEADS, blocks, STRETCH).transpose(1, 0, 2)
    cumulative = jnp.cumsum(log_decay.reshape(HEADS, blocks, STRETCH), axis=2).transpose(1, 0, 2)
    location_values = jnp.arange(STRETCH, dtype=jnp.int32)
    causal = location_values[:, None] >= location_values[None, :]

    def advance(carry_state, pieces):
        block_in, block_keys, block_queries, block_steps, block_cum = pieces
        scores = jnp.dot(block_queries, block_keys.T, preferred_element_type=jnp.float32)
        spread = block_cum[:, :, None] - block_cum[:, None, :]
        decays = jnp.where(causal[None], jnp.exp(jnp.where(causal[None], spread, 0.0)), 0.0)
        mixing = (scores[None] * decays * block_steps[:, None, :]).astype(jnp.bfloat16)
        local_out = jnp.einsum('hij,jhp->ihp', mixing.astype(jnp.float32), block_in.astype(jnp.float32))
        tail_scale = jnp.exp(block_cum[:, -1:] - block_cum) * block_steps
        weighted = (block_in.astype(jnp.float32) * tail_scale.T[:, :, None]).astype(jnp.bfloat16)
        block_state = jnp.einsum('jhp,jn->hpn', weighted.astype(jnp.float32), block_keys.astype(jnp.float32))
        carried = jnp.einsum('in,hpn->ihp', block_queries.astype(jnp.float32), carry_state, precision=lax.Precision.HIGHEST)
        carried = carried * jnp.exp(block_cum).T[:, :, None]
        result = local_out + carried + skip_gain[None, :, None] * block_in.astype(jnp.float32)
        following = jnp.exp(block_cum[:, -1])[:, None, None] * carry_state + block_state
        return (following, result)
    zero_state = jnp.zeros((HEADS, HEAD_DIM, STATE), jnp.float32)
    last_state, results = lax.scan(advance, zero_state, (inputs, key_rows, queries, step_rows, cumulative))
    return results.reshape(TOKENS, HEADS * HEAD_DIM)

def reference(mixer_input, gate_input, write_keys, read_queries, step_size, log_decay, skip_gain, out_weight, residual, norm_gain, routes, route_weight, expert_gate, expert_up, expert_down):
    result = mixer_blocks(mixer_input, write_keys, read_queries, step_size, log_decay, skip_gain)
    gated_out = (result * jax.nn.silu(gate_input.astype(jnp.float32))).astype(jnp.bfloat16)
    group_width = HEADS * HEAD_DIM // N_EXP

    def add_group(running, group_index):
        columns = lax.dynamic_slice_in_dim(gated_out, group_index * group_width, group_width, 1)
        weight_rows = lax.dynamic_slice_in_dim(out_weight, group_index * group_width, group_width, 0)
        group_term = jnp.dot(columns, weight_rows, preferred_element_type=jnp.float32).astype(jnp.bfloat16)
        group_term = lax.optimization_barrier(group_term)
        return (running + group_term.astype(jnp.float32), None)
    mixer_out = lax.scan(add_group, jnp.zeros((TOKENS, D), jnp.float32), jnp.arange(N_EXP, dtype=jnp.int32))[0]
    stream = (residual.astype(jnp.float32) + mixer_out).astype(jnp.bfloat16)
    widened = stream.astype(jnp.float32)
    normed = (widened * lax.rsqrt(lax.optimization_barrier(jnp.mean(widened * widened, axis=-1, keepdims=True)) + 1e-06) * norm_gain).astype(jnp.bfloat16)
    flat_routes = routes.reshape(-1)
    owner_row = jnp.arange(TOKENS * TOP, dtype=jnp.int32) // TOP
    flat_weight = route_weight.reshape(-1)
    most_rows = TOKENS // ROWS * CAP
    slots = jnp.arange(most_rows, dtype=jnp.int32)

    def add_expert(expert_sum, expert_index):
        chosen = flat_routes == expert_index
        picked = jnp.nonzero(chosen, size=most_rows, fill_value=0)[0].astype(jnp.int32)
        live_rows = slots < jnp.sum(chosen.astype(jnp.int32))
        token_rows = owner_row[picked]
        expert_in = normed[token_rows]
        gate_rows = lax.dynamic_slice_in_dim(expert_gate, expert_index * SPLIT, SPLIT, 0)
        up_rows = lax.dynamic_slice_in_dim(expert_up, expert_index * SPLIT, SPLIT, 0)
        down_rows = lax.dynamic_slice_in_dim(expert_down, expert_index * SPLIT, SPLIT, 0)
        combined = jnp.zeros((most_rows, D), jnp.float32)
        for piece_index in range(SPLIT):
            gate_val = jnp.dot(expert_in, gate_rows[piece_index].T, preferred_element_type=jnp.float32)
            up_val = jnp.dot(expert_in, up_rows[piece_index].T, preferred_element_type=jnp.float32)
            activated = (jax.nn.silu(gate_val) * up_val).astype(jnp.bfloat16)
            piece_out = jnp.dot(activated, down_rows[piece_index], preferred_element_type=jnp.float32).astype(jnp.bfloat16)
            combined = combined + lax.optimization_barrier(piece_out).astype(jnp.float32)
        weighting = jnp.where(live_rows, flat_weight[picked], 0.0)
        return (expert_sum.at[token_rows].add(combined * weighting[:, None]), None)
    expert_sum = lax.scan(add_expert, jnp.zeros((TOKENS, D), jnp.float32), jnp.arange(EXPERTS, dtype=jnp.int32))[0]
    return (stream.astype(jnp.float32) + expert_sum).astype(jnp.bfloat16)
```

```python
import jax
import jax.numpy as jnp
from jax import lax
from jax.sharding import Mesh, PartitionSpec as P

HEAD_DIM = 64
STATE = 128
TOP = 6
SPLIT = 4
STRETCH = 256
EXP = ("eh", "pz", "c")


def prefix(shard, axis, join, neutral):
    place = lax.axis_index(axis)
    decay, state = shard
    packed = jnp.concatenate(
        [state.reshape(state.shape[0], -1), jnp.broadcast_to(decay[:, None], (decay.shape[0], STATE))],
        axis=1,
    )
    gathered = lax.all_gather(packed.astype(jnp.bfloat16), axis)
    cut = state.shape[1] * state.shape[2]
    gathered = (gathered[:, :, cut], gathered[:, :, :cut].reshape((-1,) + state.shape))
    start = jax.tree.map(lambda a, e: jnp.zeros_like(a) + jnp.asarray(e, a.dtype), shard, neutral)

    def one(turn, carry):
        return join(
            carry,
            jax.tree.map(
                lambda a, own: lax.dynamic_index_in_dim(a, turn, 0, False).astype(own.dtype),
                gathered,
                shard,
            ),
        )

    return lax.fori_loop(0, place, one, start)


def join_states(earlier, later_part):
    return (
        earlier[0] + later_part[0],
        jnp.exp(later_part[0])[:, None, None] * earlier[1] + later_part[1],
    )


def shards(
    mixer_input,
    gate_input,
    write_keys,
    read_queries,
    step_size,
    log_decay,
    skip_gain,
    out_weight,
    residual,
    norm_gain,
    routes,
    route_weight,
    expert_gate,
    expert_up,
    expert_down,
):
    length = mixer_input.shape[0]
    head_count = step_size.shape[0]
    blocks = length // STRETCH
    inputs = mixer_input.reshape(blocks, STRETCH, head_count, HEAD_DIM)
    key_rows = write_keys.reshape(blocks, STRETCH, STATE)
    queries = read_queries.reshape(blocks, STRETCH, STATE)
    step_rows = step_size.reshape(head_count, blocks, STRETCH).transpose(1, 0, 2)
    cumulative = jnp.cumsum(log_decay.reshape(head_count, blocks, STRETCH), axis=2).transpose(
        1, 0, 2
    )
    location_values = jnp.arange(STRETCH, dtype=jnp.int32)
    causal = location_values[:, None] >= location_values[None, :]
    scores = jnp.einsum("cin,cjn->cij", queries, key_rows, preferred_element_type=jnp.float32)
    spread = cumulative[:, :, :, None] - cumulative[:, :, None, :]
    decays = jnp.where(causal, jnp.exp(jnp.where(causal, spread, 0.0)), 0.0)
    mixing = (scores[:, None] * decays * step_rows[:, :, None, :]).astype(jnp.bfloat16)
    local_out = jnp.einsum("chij,cjhp->cihp", mixing, inputs, preferred_element_type=jnp.float32)
    tail_scale = jnp.exp(cumulative[:, :, -1:] - cumulative) * step_rows
    weighted = (inputs.astype(jnp.float32) * tail_scale.transpose(0, 2, 1)[..., None]).astype(
        jnp.bfloat16
    )
    block_state = jnp.einsum(
        "cjhp,cjn->chpn", weighted, key_rows, preferred_element_type=jnp.float32
    )
    totals = cumulative[:, :, -1]

    def advance(carry_state, pieces):
        block_total, fresh_state = pieces
        return (jnp.exp(block_total)[:, None, None] * carry_state + fresh_state, carry_state)

    zero_state = jnp.zeros((head_count, HEAD_DIM, STATE), jnp.float32)
    end_local, entering_local = lax.scan(advance, zero_state, (totals, block_state))
    device_decay = jnp.sum(totals, axis=0)
    before = prefix(
        (device_decay, end_local), "seq", join_states, (jnp.zeros_like(device_decay), zero_state)
    )
    before_state = before[1]
    before_blocks = jnp.cumsum(totals, axis=0) - totals
    entering = jnp.exp(before_blocks)[:, :, None, None] * before_state[None] + entering_local
    carried = jnp.einsum(
        "cin,chpn->cihp", queries.astype(jnp.float32), entering, precision=lax.Precision.HIGHEST
    )
    carried = carried * jnp.exp(cumulative).transpose(0, 2, 1)[..., None]
    result = local_out + carried + skip_gain[None, None, :, None] * inputs.astype(jnp.float32)
    gated_out = (
        result.reshape(length, head_count * HEAD_DIM) * jax.nn.silu(gate_input.astype(jnp.float32))
    ).astype(jnp.bfloat16)
    row_count = residual.shape[0]
    mixer_out = lax.psum_scatter(
        jnp.dot(gated_out, out_weight, preferred_element_type=jnp.float32).astype(jnp.bfloat16),
        EXP,
        scatter_dimension=0,
        tiled=True,
    ).astype(jnp.float32)
    stream = (residual.astype(jnp.float32) + mixer_out).astype(jnp.bfloat16)
    widened = stream.astype(jnp.float32)
    normed = (
        widened * lax.rsqrt(jnp.mean(widened * widened, axis=-1, keepdims=True) + 1e-06) * norm_gain
    ).astype(jnp.bfloat16)
    seq_count = lax.axis_size("seq")
    exp_count = lax.axis_size(EXP)
    row_experts = exp_count // SPLIT
    experts = seq_count * row_experts
    capacity = min(row_count, max(2, (4 * TOP * row_count + 3 * experts - 1) // (3 * experts)))
    flat_routes = routes.reshape(-1)
    onehot = (flat_routes[:, None] == jnp.arange(experts, dtype=jnp.int32)[None, :]).astype(
        jnp.int32
    )
    earlier_count = jnp.cumsum(onehot, axis=0) - onehot
    slot_index = jnp.sum(earlier_count * onehot, axis=1)
    target = (
        flat_routes % row_experts * (seq_count * capacity)
        + flat_routes // row_experts * capacity
        + slot_index
    )
    owner_row = jnp.arange(flat_routes.shape[0], dtype=jnp.int32) // TOP
    source = jnp.zeros((experts * capacity,), jnp.int32).at[target].set(owner_row)
    filled = jnp.zeros((experts * capacity,), jnp.bool_).at[target].set(True)
    outgoing = jnp.where(filled[:, None], normed[source], jnp.zeros((), jnp.bfloat16))
    outgoing = outgoing.reshape(row_experts, seq_count, capacity, -1)
    arrived = lax.all_to_all(outgoing, "seq", split_axis=1, concat_axis=1, tiled=True)
    arrived = lax.all_to_all(arrived, "eh", split_axis=0, concat_axis=0, tiled=True)
    block = lax.all_gather(arrived, "pz")
    block = lax.all_gather(block, "c")
    flat_rows = block.reshape(-1, block.shape[-1])
    contract = (((1,), (1,)), ((), ()))
    gate_val = lax.dot_general(
        flat_rows, expert_gate[0], contract, preferred_element_type=jnp.float32
    )
    up_val = lax.dot_general(flat_rows, expert_up[0], contract, preferred_element_type=jnp.float32)
    activated = (jax.nn.silu(gate_val) * up_val).astype(jnp.bfloat16)
    piece_out = jnp.dot(activated, expert_down[0], preferred_element_type=jnp.float32).astype(
        jnp.bfloat16
    )
    piece_out = piece_out.reshape(block.shape)
    piece_sum = lax.psum_scatter(piece_out, "c", scatter_dimension=0, tiled=True)[0]
    piece_sum = lax.psum_scatter(piece_sum, "pz", scatter_dimension=0, tiled=True)[0]
    returned = lax.all_to_all(piece_sum, "eh", split_axis=0, concat_axis=0, tiled=True)
    returned = lax.all_to_all(returned, "seq", split_axis=1, concat_axis=1, tiled=True)
    summed = returned.astype(jnp.float32)
    results = summed.reshape(experts * capacity, -1)[target]
    expert_sum = jnp.sum(
        (results * route_weight.reshape(-1)[:, None]).reshape(row_count, TOP, -1), axis=1
    )
    return (stream.astype(jnp.float32) + expert_sum).astype(jnp.bfloat16)


def solution(mesh):
    seq_n = mesh.shape["seq"]
    exp_n = mesh.shape["exp"]
    grid = Mesh(mesh.devices.reshape(seq_n, exp_n // SPLIT, 2, SPLIT // 2), ("seq",) + EXP)
    return jax.shard_map(
        shards,
        mesh=grid,
        in_specs=(
            P("seq", EXP),
            P("seq", EXP),
            P("seq", None),
            P("seq", None),
            P(EXP, "seq"),
            P(EXP, "seq"),
            P(EXP),
            P(EXP, None),
            P(("seq",) + EXP, None),
            P(),
            P(("seq",) + EXP, None),
            P(("seq",) + EXP, None),
            P(("seq",) + EXP, None, None),
            P(("seq",) + EXP, None, None),
            P(("seq",) + EXP, None, None),
        ),
        out_specs=P(("seq",) + EXP, None),
        check_vma=False,
    )
```

```python
import jax
import jax.numpy as jnp
from jax import lax
from jax.sharding import Mesh, PartitionSpec as P

HEAD_DIM = 64
STATE = 128
TOP = 6
SPLIT = 4
STRETCH = 256
EXP = ("eh", "pz", "c")
JOINT = True
PZ_SWAP = True
C_SWAP = True
MIX_TWO = True


def pair_swap(x, axis):
    return lax.ppermute(x, axis, perm=[(0, 1), (1, 0)])


def pair_gather(x, axis, swap):
    if swap:
        return jnp.stack([x, pair_swap(x, axis)])
    return lax.all_gather(x, axis)


def pair_reduce(x, axis, swap):
    if swap:
        return (x[0].astype(jnp.float32) + pair_swap(x[1], axis).astype(jnp.float32)).astype(x.dtype)
    return lax.psum_scatter(x, axis, scatter_dimension=0, tiled=True)[0]


def prefix(shard, axis, join, neutral):
    place = lax.axis_index(axis)
    decay, state = shard
    packed = jnp.concatenate(
        [state.reshape(state.shape[0], -1), jnp.broadcast_to(decay[:, None], (decay.shape[0], STATE))],
        axis=1,
    )
    gathered = lax.all_gather(packed.astype(jnp.bfloat16), axis)
    cut = state.shape[1] * state.shape[2]
    gathered = (gathered[:, :, cut], gathered[:, :, :cut].reshape((-1,) + state.shape))
    start = jax.tree.map(lambda a, e: jnp.zeros_like(a) + jnp.asarray(e, a.dtype), shard, neutral)

    def one(turn, carry):
        return join(
            carry,
            jax.tree.map(
                lambda a, own: lax.dynamic_index_in_dim(a, turn, 0, False).astype(own.dtype),
                gathered,
                shard,
            ),
        )

    return lax.fori_loop(0, place, one, start)


def join_states(earlier, later_part):
    return (
        earlier[0] + later_part[0],
        jnp.exp(later_part[0])[:, None, None] * earlier[1] + later_part[1],
    )


def shards(
    mixer_input,
    gate_input,
    write_keys,
    read_queries,
    step_size,
    log_decay,
    skip_gain,
    out_weight,
    residual,
    norm_gain,
    routes,
    route_weight,
    expert_gate,
    expert_up,
    expert_down,
):
    length = mixer_input.shape[0]
    head_count = step_size.shape[0]
    blocks = length // STRETCH
    inputs = mixer_input.reshape(blocks, STRETCH, head_count, HEAD_DIM)
    key_rows = write_keys.reshape(blocks, STRETCH, STATE)
    queries = read_queries.reshape(blocks, STRETCH, STATE)
    step_rows = step_size.reshape(head_count, blocks, STRETCH).transpose(1, 0, 2)
    cumulative = jnp.cumsum(log_decay.reshape(head_count, blocks, STRETCH), axis=2).transpose(
        1, 0, 2
    )
    location_values = jnp.arange(STRETCH, dtype=jnp.int32)
    causal = location_values[:, None] >= location_values[None, :]
    scores = jnp.einsum("cin,cjn->cij", queries, key_rows, preferred_element_type=jnp.float32)
    spread = cumulative[:, :, :, None] - cumulative[:, :, None, :]
    decays = jnp.where(causal, jnp.exp(jnp.where(causal, spread, 0.0)), 0.0)
    mixing = (scores[:, None] * decays * step_rows[:, :, None, :]).astype(jnp.bfloat16)
    local_out = jnp.einsum("chij,cjhp->cihp", mixing, inputs, preferred_element_type=jnp.float32)
    tail_scale = jnp.exp(cumulative[:, :, -1:] - cumulative) * step_rows
    weighted = (inputs.astype(jnp.float32) * tail_scale.transpose(0, 2, 1)[..., None]).astype(
        jnp.bfloat16
    )
    block_state = jnp.einsum(
        "cjhp,cjn->chpn", weighted, key_rows, preferred_element_type=jnp.float32
    )
    totals = cumulative[:, :, -1]

    def advance(carry_state, pieces):
        block_total, fresh_state = pieces
        return (jnp.exp(block_total)[:, None, None] * carry_state + fresh_state, carry_state)

    zero_state = jnp.zeros((head_count, HEAD_DIM, STATE), jnp.float32)
    end_local, entering_local = lax.scan(advance, zero_state, (totals, block_state))
    device_decay = jnp.sum(totals, axis=0)
    before = prefix(
        (device_decay, end_local), "seq", join_states, (jnp.zeros_like(device_decay), zero_state)
    )
    before_state = before[1]
    before_blocks = jnp.cumsum(totals, axis=0) - totals
    entering = jnp.exp(before_blocks)[:, :, None, None] * before_state[None] + entering_local
    carried = jnp.einsum(
        "cin,chpn->cihp", queries.astype(jnp.float32), entering, precision=lax.Precision.HIGHEST
    )
    carried = carried * jnp.exp(cumulative).transpose(0, 2, 1)[..., None]
    result = local_out + carried + skip_gain[None, None, :, None] * inputs.astype(jnp.float32)
    gated_out = (
        result.reshape(length, head_count * HEAD_DIM) * jax.nn.silu(gate_input.astype(jnp.float32))
    ).astype(jnp.bfloat16)
    row_count = residual.shape[0]
    projected = jnp.dot(gated_out, out_weight, preferred_element_type=jnp.float32).astype(
        jnp.bfloat16
    )
    if MIX_TWO:
        cores = lax.axis_size("c")
        projected = projected.reshape(-1, cores, row_count, projected.shape[-1]).transpose(1, 0, 2, 3)
        projected = lax.psum_scatter(projected, "c", scatter_dimension=0, tiled=True)[0]
        mixer_out = lax.psum_scatter(
            projected, ("eh", "pz"), scatter_dimension=0, tiled=True
        )[0].astype(jnp.float32)
    else:
        mixer_out = lax.psum_scatter(projected, EXP, scatter_dimension=0, tiled=True).astype(
            jnp.float32
        )
    stream = (residual.astype(jnp.float32) + mixer_out).astype(jnp.bfloat16)
    widened = stream.astype(jnp.float32)
    normed = (
        widened * lax.rsqrt(jnp.mean(widened * widened, axis=-1, keepdims=True) + 1e-06) * norm_gain
    ).astype(jnp.bfloat16)
    seq_count = lax.axis_size("seq")
    exp_count = lax.axis_size(EXP)
    row_experts = exp_count // SPLIT
    experts = seq_count * row_experts
    capacity = min(row_count, max(2, (4 * TOP * row_count + 3 * experts - 1) // (3 * experts)))
    flat_routes = routes.reshape(-1)
    onehot = (flat_routes[:, None] == jnp.arange(experts, dtype=jnp.int32)[None, :]).astype(
        jnp.int32
    )
    earlier_count = jnp.cumsum(onehot, axis=0) - onehot
    slot_index = jnp.sum(earlier_count * onehot, axis=1)
    if JOINT:
        target = flat_routes * capacity + slot_index
    else:
        target = (
            flat_routes % row_experts * (seq_count * capacity)
            + flat_routes // row_experts * capacity
            + slot_index
        )
    owner_row = jnp.arange(flat_routes.shape[0], dtype=jnp.int32) // TOP
    source = jnp.zeros((experts * capacity,), jnp.int32).at[target].set(owner_row)
    filled = jnp.zeros((experts * capacity,), jnp.bool_).at[target].set(True)
    outgoing = jnp.where(filled[:, None], normed[source], jnp.zeros((), jnp.bfloat16))
    if JOINT:
        outgoing = outgoing.reshape(experts, capacity, -1)
        arrived = lax.all_to_all(outgoing, ("seq", "eh"), split_axis=0, concat_axis=0, tiled=True)
    else:
        outgoing = outgoing.reshape(row_experts, seq_count, capacity, -1)
        arrived = lax.all_to_all(outgoing, "seq", split_axis=1, concat_axis=1, tiled=True)
        arrived = lax.all_to_all(arrived, "eh", split_axis=0, concat_axis=0, tiled=True)
    block = pair_gather(arrived, "pz", PZ_SWAP)
    block = pair_gather(block, "c", C_SWAP)
    flat_rows = block.reshape(-1, block.shape[-1])
    contract = (((1,), (1,)), ((), ()))
    gate_val = lax.dot_general(
        flat_rows, expert_gate[0], contract, preferred_element_type=jnp.float32
    )
    up_val = lax.dot_general(flat_rows, expert_up[0], contract, preferred_element_type=jnp.float32)
    activated = (jax.nn.silu(gate_val) * up_val).astype(jnp.bfloat16)
    piece_out = jnp.dot(activated, expert_down[0], preferred_element_type=jnp.float32).astype(
        jnp.bfloat16
    )
    piece_out = piece_out.reshape(block.shape)
    piece_sum = pair_reduce(piece_out, "c", C_SWAP)
    piece_sum = pair_reduce(piece_sum, "pz", PZ_SWAP)
    if JOINT:
        returned = lax.all_to_all(piece_sum, ("seq", "eh"), split_axis=0, concat_axis=0, tiled=True)
    else:
        returned = lax.all_to_all(piece_sum, "eh", split_axis=0, concat_axis=0, tiled=True)
        returned = lax.all_to_all(returned, "seq", split_axis=1, concat_axis=1, tiled=True)
    summed = returned.astype(jnp.float32)
    results = summed.reshape(experts * capacity, -1)[target]
    expert_sum = jnp.sum(
        (results * route_weight.reshape(-1)[:, None]).reshape(row_count, TOP, -1), axis=1
    )
    return (stream.astype(jnp.float32) + expert_sum).astype(jnp.bfloat16)


def solution(mesh):
    seq_n = mesh.shape["seq"]
    exp_n = mesh.shape["exp"]
    grid = Mesh(mesh.devices.reshape(seq_n, exp_n // SPLIT, 2, SPLIT // 2), ("seq",) + EXP)
    return jax.shard_map(
        shards,
        mesh=grid,
        in_specs=(
            P("seq", EXP),
            P("seq", EXP),
            P("seq", None),
            P("seq", None),
            P(EXP, "seq"),
            P(EXP, "seq"),
            P(EXP),
            P(EXP, None),
            P(("seq",) + EXP, None),
            P(),
            P(("seq",) + EXP, None),
            P(("seq",) + EXP, None),
            P(("seq",) + EXP, None, None),
            P(("seq",) + EXP, None, None),
            P(("seq",) + EXP, None, None),
        ),
        out_specs=P(("seq",) + EXP, None),
        check_vma=False,
    )
```

```python
import jax
import jax.numpy as jnp
from jax import lax
from jax.sharding import Mesh, PartitionSpec as P

HEAD_DIM = 64
STATE = 128
TOP = 6
SPLIT = 4
STRETCH = 256
EXP = ("eh", "pz", "c")
JOINT = True
PZ_SWAP = True
C_SWAP = True
MIX_TWO = True
MIX_SWAP = True
PREFIX_SCAN = True


def scan_prefix(decay, state, axis):
    count = lax.axis_size(axis)
    cut = state.shape[1] * state.shape[2]
    heads = state.shape[0]

    def split(packed):
        return packed[:, cut], packed[:, :cut].reshape(state.shape)

    def join(earlier, later):
        early_decay, early_state = split(earlier)
        late_decay, late_state = split(later)
        total = early_decay + late_decay
        carried = jnp.exp(late_decay)[:, None, None] * early_state + late_state
        return jnp.concatenate(
            [carried.reshape(heads, cut), jnp.broadcast_to(total[:, None], (heads, STATE))], axis=1
        )

    packed = jnp.concatenate(
        [state.reshape(heads, cut), jnp.broadcast_to(decay[:, None], (heads, STATE))], axis=1
    )
    packed = lax.ppermute(packed, axis, perm=[(i, i + 1) for i in range(count - 1)])
    shift = 1
    while shift < count:
        moved = lax.ppermute(packed, axis, perm=[(i, i + shift) for i in range(count - shift)])
        packed = join(moved, packed)
        shift *= 2
    return split(packed)


def pair_swap(x, axis):
    return lax.ppermute(x, axis, perm=[(0, 1), (1, 0)])


def pair_gather(x, axis, swap):
    if swap:
        return jnp.stack([x, pair_swap(x, axis)])
    return lax.all_gather(x, axis)


def pair_reduce(x, axis, swap):
    if swap:
        return (x[0].astype(jnp.float32) + pair_swap(x[1], axis).astype(jnp.float32)).astype(x.dtype)
    return lax.psum_scatter(x, axis, scatter_dimension=0, tiled=True)[0]


def prefix(shard, axis, join, neutral):
    place = lax.axis_index(axis)
    decay, state = shard
    packed = jnp.concatenate(
        [state.reshape(state.shape[0], -1), jnp.broadcast_to(decay[:, None], (decay.shape[0], STATE))],
        axis=1,
    )
    gathered = lax.all_gather(packed.astype(jnp.bfloat16), axis)
    cut = state.shape[1] * state.shape[2]
    gathered = (gathered[:, :, cut], gathered[:, :, :cut].reshape((-1,) + state.shape))
    start = jax.tree.map(lambda a, e: jnp.zeros_like(a) + jnp.asarray(e, a.dtype), shard, neutral)

    def one(turn, carry):
        return join(
            carry,
            jax.tree.map(
                lambda a, own: lax.dynamic_index_in_dim(a, turn, 0, False).astype(own.dtype),
                gathered,
                shard,
            ),
        )

    return lax.fori_loop(0, place, one, start)


def join_states(earlier, later_part):
    return (
        earlier[0] + later_part[0],
        jnp.exp(later_part[0])[:, None, None] * earlier[1] + later_part[1],
    )


def shards(
    mixer_input,
    gate_input,
    write_keys,
    read_queries,
    step_size,
    log_decay,
    skip_gain,
    out_weight,
    residual,
    norm_gain,
    routes,
    route_weight,
    expert_gate,
    expert_up,
    expert_down,
):
    length = mixer_input.shape[0]
    head_count = step_size.shape[0]
    blocks = length // STRETCH
    inputs = mixer_input.reshape(blocks, STRETCH, head_count, HEAD_DIM)
    key_rows = write_keys.reshape(blocks, STRETCH, STATE)
    queries = read_queries.reshape(blocks, STRETCH, STATE)
    step_rows = step_size.reshape(head_count, blocks, STRETCH).transpose(1, 0, 2)
    cumulative = jnp.cumsum(log_decay.reshape(head_count, blocks, STRETCH), axis=2).transpose(
        1, 0, 2
    )
    location_values = jnp.arange(STRETCH, dtype=jnp.int32)
    causal = location_values[:, None] >= location_values[None, :]
    scores = jnp.einsum("cin,cjn->cij", queries, key_rows, preferred_element_type=jnp.float32)
    spread = cumulative[:, :, :, None] - cumulative[:, :, None, :]
    decays = jnp.where(causal, jnp.exp(jnp.where(causal, spread, 0.0)), 0.0)
    mixing = (scores[:, None] * decays * step_rows[:, :, None, :]).astype(jnp.bfloat16)
    local_out = jnp.einsum("chij,cjhp->cihp", mixing, inputs, preferred_element_type=jnp.float32)
    tail_scale = jnp.exp(cumulative[:, :, -1:] - cumulative) * step_rows
    weighted = (inputs.astype(jnp.float32) * tail_scale.transpose(0, 2, 1)[..., None]).astype(
        jnp.bfloat16
    )
    block_state = jnp.einsum(
        "cjhp,cjn->chpn", weighted, key_rows, preferred_element_type=jnp.float32
    )
    totals = cumulative[:, :, -1]

    def advance(carry_state, pieces):
        block_total, fresh_state = pieces
        return (jnp.exp(block_total)[:, None, None] * carry_state + fresh_state, carry_state)

    zero_state = jnp.zeros((head_count, HEAD_DIM, STATE), jnp.float32)
    end_local, entering_local = lax.scan(advance, zero_state, (totals, block_state))
    device_decay = jnp.sum(totals, axis=0)
    if PREFIX_SCAN:
        before = scan_prefix(device_decay, end_local, "seq")
    else:
        before = prefix(
            (device_decay, end_local), "seq", join_states, (jnp.zeros_like(device_decay), zero_state)
        )
    before_state = before[1]
    before_blocks = jnp.cumsum(totals, axis=0) - totals
    entering = jnp.exp(before_blocks)[:, :, None, None] * before_state[None] + entering_local
    carried = jnp.einsum(
        "cin,chpn->cihp", queries.astype(jnp.float32), entering, precision=lax.Precision.HIGHEST
    )
    carried = carried * jnp.exp(cumulative).transpose(0, 2, 1)[..., None]
    result = local_out + carried + skip_gain[None, None, :, None] * inputs.astype(jnp.float32)
    gated_out = (
        result.reshape(length, head_count * HEAD_DIM) * jax.nn.silu(gate_input.astype(jnp.float32))
    ).astype(jnp.bfloat16)
    row_count = residual.shape[0]
    projected = jnp.dot(gated_out, out_weight, preferred_element_type=jnp.float32).astype(
        jnp.bfloat16
    )
    if MIX_TWO:
        cores = lax.axis_size("c")
        projected = projected.reshape(-1, cores, row_count, projected.shape[-1]).transpose(1, 0, 2, 3)
        if MIX_SWAP:
            core = lax.axis_index("c")
            projected = pair_reduce(
                jnp.stack(
                    [
                        lax.dynamic_index_in_dim(projected, core, 0, False),
                        lax.dynamic_index_in_dim(projected, 1 - core, 0, False),
                    ]
                ),
                "c",
                True,
            )
        else:
            projected = lax.psum_scatter(projected, "c", scatter_dimension=0, tiled=True)[0]
        mixer_out = lax.psum_scatter(
            projected, ("eh", "pz"), scatter_dimension=0, tiled=True
        )[0].astype(jnp.float32)
    else:
        mixer_out = lax.psum_scatter(projected, EXP, scatter_dimension=0, tiled=True).astype(
            jnp.float32
        )
    stream = (residual.astype(jnp.float32) + mixer_out).astype(jnp.bfloat16)
    widened = stream.astype(jnp.float32)
    normed = (
        widened * lax.rsqrt(jnp.mean(widened * widened, axis=-1, keepdims=True) + 1e-06) * norm_gain
    ).astype(jnp.bfloat16)
    seq_count = lax.axis_size("seq")
    exp_count = lax.axis_size(EXP)
    row_experts = exp_count // SPLIT
    experts = seq_count * row_experts
    capacity = min(row_count, max(2, (4 * TOP * row_count + 3 * experts - 1) // (3 * experts)))
    flat_routes = routes.reshape(-1)
    onehot = (flat_routes[:, None] == jnp.arange(experts, dtype=jnp.int32)[None, :]).astype(
        jnp.int32
    )
    earlier_count = jnp.cumsum(onehot, axis=0) - onehot
    slot_index = jnp.sum(earlier_count * onehot, axis=1)
    if JOINT:
        target = flat_routes * capacity + slot_index
    else:
        target = (
            flat_routes % row_experts * (seq_count * capacity)
            + flat_routes // row_experts * capacity
            + slot_index
        )
    owner_row = jnp.arange(flat_routes.shape[0], dtype=jnp.int32) // TOP
    source = jnp.zeros((experts * capacity,), jnp.int32).at[target].set(owner_row)
    filled = jnp.zeros((experts * capacity,), jnp.bool_).at[target].set(True)
    outgoing = jnp.where(filled[:, None], normed[source], jnp.zeros((), jnp.bfloat16))
    if JOINT:
        outgoing = outgoing.reshape(experts, capacity, -1)
        arrived = lax.all_to_all(outgoing, ("seq", "eh"), split_axis=0, concat_axis=0, tiled=True)
    else:
        outgoing = outgoing.reshape(row_experts, seq_count, capacity, -1)
        arrived = lax.all_to_all(outgoing, "seq", split_axis=1, concat_axis=1, tiled=True)
        arrived = lax.all_to_all(arrived, "eh", split_axis=0, concat_axis=0, tiled=True)
    block = pair_gather(arrived, "pz", PZ_SWAP)
    block = pair_gather(block, "c", C_SWAP)
    flat_rows = block.reshape(-1, block.shape[-1])
    contract = (((1,), (1,)), ((), ()))
    gate_val = lax.dot_general(
        flat_rows, expert_gate[0], contract, preferred_element_type=jnp.float32
    )
    up_val = lax.dot_general(flat_rows, expert_up[0], contract, preferred_element_type=jnp.float32)
    activated = (jax.nn.silu(gate_val) * up_val).astype(jnp.bfloat16)
    piece_out = jnp.dot(activated, expert_down[0], preferred_element_type=jnp.float32).astype(
        jnp.bfloat16
    )
    piece_out = piece_out.reshape(block.shape)
    piece_sum = pair_reduce(piece_out, "c", C_SWAP)
    piece_sum = pair_reduce(piece_sum, "pz", PZ_SWAP)
    if JOINT:
        returned = lax.all_to_all(piece_sum, ("seq", "eh"), split_axis=0, concat_axis=0, tiled=True)
    else:
        returned = lax.all_to_all(piece_sum, "eh", split_axis=0, concat_axis=0, tiled=True)
        returned = lax.all_to_all(returned, "seq", split_axis=1, concat_axis=1, tiled=True)
    summed = returned.astype(jnp.float32)
    results = summed.reshape(experts * capacity, -1)[target]
    expert_sum = jnp.sum(
        (results * route_weight.reshape(-1)[:, None]).reshape(row_count, TOP, -1), axis=1
    )
    return (stream.astype(jnp.float32) + expert_sum).astype(jnp.bfloat16)


def solution(mesh):
    seq_n = mesh.shape["seq"]
    exp_n = mesh.shape["exp"]
    grid = Mesh(mesh.devices.reshape(seq_n, exp_n // SPLIT, 2, SPLIT // 2), ("seq",) + EXP)
    return jax.shard_map(
        shards,
        mesh=grid,
        in_specs=(
            P("seq", EXP),
            P("seq", EXP),
            P("seq", None),
            P("seq", None),
            P(EXP, "seq"),
            P(EXP, "seq"),
            P(EXP),
            P(EXP, None),
            P(("seq",) + EXP, None),
            P(),
            P(("seq",) + EXP, None),
            P(("seq",) + EXP, None),
            P(("seq",) + EXP, None, None),
            P(("seq",) + EXP, None, None),
            P(("seq",) + EXP, None, None),
        ),
        out_specs=P(("seq",) + EXP, None),
        check_vma=False,
    )
```

```python
import jax
import jax.numpy as jnp
from jax import lax
from jax.sharding import Mesh, PartitionSpec as P

HEAD_DIM = 64
STATE = 128
TOP = 6
SPLIT = 4
STRETCH = 256
EXP = ("eh", "pz", "c")
PZ_SWAP = True
C_SWAP = True
MIX_TWO = True
MIX_SWAP = True
PREFIX_SCAN = True
CHUNKS = 1
SCAN4 = True
ONEHOT = True


def radix_prefix(decay, state, axis):
    heads = state.shape[0]
    cut = state.shape[1] * state.shape[2]

    def join(earlier, later):
        total = earlier[:, cut] + later[:, cut]
        carried = jnp.exp(later[:, cut])[:, None] * earlier[:, :cut] + later[:, :cut]
        return jnp.concatenate([carried, jnp.broadcast_to(total[:, None], (heads, STATE))], axis=1)

    def shifted(packed, shift):
        count = lax.axis_size(axis)
        return lax.ppermute(packed, axis, perm=[(i, i + shift) for i in range(count - shift)])

    own = jnp.concatenate(
        [state.reshape(heads, cut), jnp.broadcast_to(decay[:, None], (heads, STATE))], axis=1
    )
    window = join(shifted(own, 3), join(shifted(own, 2), shifted(own, 1)))
    span = join(window, own)
    result = join(shifted(span, 12), join(shifted(span, 8), join(shifted(span, 4), window)))
    return result[:, cut], result[:, :cut].reshape(state.shape)


def expert_round(outgoing, expert_gate, expert_up, expert_down):
    arrived = lax.all_to_all(outgoing, ("seq", "eh"), split_axis=0, concat_axis=0, tiled=True)
    block = pair_gather(arrived, "pz", PZ_SWAP)
    block = pair_gather(block, "c", C_SWAP)
    flat_rows = block.reshape(-1, block.shape[-1])
    contract = (((1,), (1,)), ((), ()))
    gate_val = lax.dot_general(
        flat_rows, expert_gate[0], contract, preferred_element_type=jnp.float32
    )
    up_val = lax.dot_general(flat_rows, expert_up[0], contract, preferred_element_type=jnp.float32)
    activated = (jax.nn.silu(gate_val) * up_val).astype(jnp.bfloat16)
    piece_out = jnp.dot(activated, expert_down[0], preferred_element_type=jnp.float32).astype(
        jnp.bfloat16
    )
    piece_out = piece_out.reshape(block.shape)
    piece_sum = pair_reduce(piece_out, "c", C_SWAP)
    piece_sum = pair_reduce(piece_sum, "pz", PZ_SWAP)
    return lax.all_to_all(piece_sum, ("seq", "eh"), split_axis=0, concat_axis=0, tiled=True)


def scan_prefix(decay, state, axis):
    count = lax.axis_size(axis)
    cut = state.shape[1] * state.shape[2]
    heads = state.shape[0]

    def split(packed):
        return packed[:, cut], packed[:, :cut].reshape(state.shape)

    def join(earlier, later):
        early_decay, early_state = split(earlier)
        late_decay, late_state = split(later)
        total = early_decay + late_decay
        carried = jnp.exp(late_decay)[:, None, None] * early_state + late_state
        return jnp.concatenate(
            [carried.reshape(heads, cut), jnp.broadcast_to(total[:, None], (heads, STATE))], axis=1
        )

    packed = jnp.concatenate(
        [state.reshape(heads, cut), jnp.broadcast_to(decay[:, None], (heads, STATE))], axis=1
    )
    packed = lax.ppermute(packed, axis, perm=[(i, i + 1) for i in range(count - 1)])
    shift = 1
    while shift < count:
        moved = lax.ppermute(packed, axis, perm=[(i, i + shift) for i in range(count - shift)])
        packed = join(moved, packed)
        shift *= 2
    return split(packed)


def pair_swap(x, axis):
    return lax.ppermute(x, axis, perm=[(0, 1), (1, 0)])


def pair_gather(x, axis, swap):
    if swap:
        return jnp.stack([x, pair_swap(x, axis)])
    return lax.all_gather(x, axis)


def pair_reduce(x, axis, swap):
    if swap:
        return (x[0].astype(jnp.float32) + pair_swap(x[1], axis).astype(jnp.float32)).astype(x.dtype)
    return lax.psum_scatter(x, axis, scatter_dimension=0, tiled=True)[0]


def prefix(shard, axis, join, neutral):
    place = lax.axis_index(axis)
    decay, state = shard
    packed = jnp.concatenate(
        [state.reshape(state.shape[0], -1), jnp.broadcast_to(decay[:, None], (decay.shape[0], STATE))],
        axis=1,
    )
    gathered = lax.all_gather(packed.astype(jnp.bfloat16), axis)
    cut = state.shape[1] * state.shape[2]
    gathered = (gathered[:, :, cut], gathered[:, :, :cut].reshape((-1,) + state.shape))
    start = jax.tree.map(lambda a, e: jnp.zeros_like(a) + jnp.asarray(e, a.dtype), shard, neutral)

    def one(turn, carry):
        return join(
            carry,
            jax.tree.map(
                lambda a, own: lax.dynamic_index_in_dim(a, turn, 0, False).astype(own.dtype),
                gathered,
                shard,
            ),
        )

    return lax.fori_loop(0, place, one, start)


def join_states(earlier, later_part):
    return (
        earlier[0] + later_part[0],
        jnp.exp(later_part[0])[:, None, None] * earlier[1] + later_part[1],
    )


def shards(
    mixer_input,
    gate_input,
    write_keys,
    read_queries,
    step_size,
    log_decay,
    skip_gain,
    out_weight,
    residual,
    norm_gain,
    routes,
    route_weight,
    expert_gate,
    expert_up,
    expert_down,
):
    length = mixer_input.shape[0]
    head_count = step_size.shape[0]
    blocks = length // STRETCH
    inputs = mixer_input.reshape(blocks, STRETCH, head_count, HEAD_DIM)
    key_rows = write_keys.reshape(blocks, STRETCH, STATE)
    queries = read_queries.reshape(blocks, STRETCH, STATE)
    step_rows = step_size.reshape(head_count, blocks, STRETCH).transpose(1, 0, 2)
    cumulative = jnp.cumsum(log_decay.reshape(head_count, blocks, STRETCH), axis=2).transpose(
        1, 0, 2
    )
    location_values = jnp.arange(STRETCH, dtype=jnp.int32)
    causal = location_values[:, None] >= location_values[None, :]
    scores = jnp.einsum("cin,cjn->cij", queries, key_rows, preferred_element_type=jnp.float32)
    spread = cumulative[:, :, :, None] - cumulative[:, :, None, :]
    decays = jnp.where(causal, jnp.exp(jnp.where(causal, spread, 0.0)), 0.0)
    mixing = (scores[:, None] * decays * step_rows[:, :, None, :]).astype(jnp.bfloat16)
    local_out = jnp.einsum("chij,cjhp->cihp", mixing, inputs, preferred_element_type=jnp.float32)
    tail_scale = jnp.exp(cumulative[:, :, -1:] - cumulative) * step_rows
    weighted = (inputs.astype(jnp.float32) * tail_scale.transpose(0, 2, 1)[..., None]).astype(
        jnp.bfloat16
    )
    block_state = jnp.einsum(
        "cjhp,cjn->chpn", weighted, key_rows, preferred_element_type=jnp.float32
    )
    totals = cumulative[:, :, -1]

    def advance(carry_state, pieces):
        block_total, fresh_state = pieces
        return (jnp.exp(block_total)[:, None, None] * carry_state + fresh_state, carry_state)

    zero_state = jnp.zeros((head_count, HEAD_DIM, STATE), jnp.float32)
    end_local, entering_local = lax.scan(advance, zero_state, (totals, block_state))
    device_decay = jnp.sum(totals, axis=0)
    if SCAN4 and lax.axis_size("seq") <= 16:
        before = radix_prefix(device_decay, end_local, "seq")
    elif PREFIX_SCAN:
        before = scan_prefix(device_decay, end_local, "seq")
    else:
        before = prefix(
            (device_decay, end_local), "seq", join_states, (jnp.zeros_like(device_decay), zero_state)
        )
    before_state = before[1]
    before_blocks = jnp.cumsum(totals, axis=0) - totals
    entering = jnp.exp(before_blocks)[:, :, None, None] * before_state[None] + entering_local
    carried = jnp.einsum(
        "cin,chpn->cihp", queries.astype(jnp.float32), entering, precision=lax.Precision.HIGHEST
    )
    carried = carried * jnp.exp(cumulative).transpose(0, 2, 1)[..., None]
    result = local_out + carried + skip_gain[None, None, :, None] * inputs.astype(jnp.float32)
    gated_out = (
        result.reshape(length, head_count * HEAD_DIM) * jax.nn.silu(gate_input.astype(jnp.float32))
    ).astype(jnp.bfloat16)
    row_count = residual.shape[0]
    projected = jnp.dot(gated_out, out_weight, preferred_element_type=jnp.float32).astype(
        jnp.bfloat16
    )
    if MIX_TWO:
        cores = lax.axis_size("c")
        projected = projected.reshape(-1, cores, row_count, projected.shape[-1]).transpose(1, 0, 2, 3)
        if MIX_SWAP:
            core = lax.axis_index("c")
            projected = pair_reduce(
                jnp.stack(
                    [
                        lax.dynamic_index_in_dim(projected, core, 0, False),
                        lax.dynamic_index_in_dim(projected, 1 - core, 0, False),
                    ]
                ),
                "c",
                True,
            )
        else:
            projected = lax.psum_scatter(projected, "c", scatter_dimension=0, tiled=True)[0]
        mixer_out = lax.psum_scatter(
            projected, ("eh", "pz"), scatter_dimension=0, tiled=True
        )[0].astype(jnp.float32)
    else:
        mixer_out = lax.psum_scatter(projected, EXP, scatter_dimension=0, tiled=True).astype(
            jnp.float32
        )
    stream = (residual.astype(jnp.float32) + mixer_out).astype(jnp.bfloat16)
    widened = stream.astype(jnp.float32)
    normed = (
        widened * lax.rsqrt(jnp.mean(widened * widened, axis=-1, keepdims=True) + 1e-06) * norm_gain
    ).astype(jnp.bfloat16)
    seq_count = lax.axis_size("seq")
    exp_count = lax.axis_size(EXP)
    row_experts = exp_count // SPLIT
    experts = seq_count * row_experts
    capacity = min(row_count, max(2, (4 * TOP * row_count + 3 * experts - 1) // (3 * experts)))
    flat_routes = routes.reshape(-1)
    onehot = (flat_routes[:, None] == jnp.arange(experts, dtype=jnp.int32)[None, :]).astype(
        jnp.int32
    )
    earlier_count = jnp.cumsum(onehot, axis=0) - onehot
    slot_index = jnp.sum(earlier_count * onehot, axis=1)
    target = flat_routes * capacity + slot_index
    owner_row = jnp.arange(flat_routes.shape[0], dtype=jnp.int32) // TOP
    source = jnp.zeros((experts * capacity,), jnp.int32).at[target].set(owner_row)
    filled = jnp.zeros((experts * capacity,), jnp.bool_).at[target].set(True)
    slots = jnp.arange(experts * capacity, dtype=jnp.int32)
    hits = target.reshape(row_count, TOP)[:, :, None] == slots[None, None, :]
    if ONEHOT:
        picks = jnp.any(hits, axis=1).T.astype(jnp.bfloat16)
        outgoing = jnp.dot(picks, normed, preferred_element_type=jnp.float32).astype(jnp.bfloat16)
    else:
        outgoing = jnp.where(filled[:, None], normed[source], jnp.zeros((), jnp.bfloat16))
    outgoing = outgoing.reshape(experts, capacity, -1)
    step = capacity // CHUNKS
    returned = jnp.concatenate(
        [
            expert_round(outgoing[:, part * step : (part + 1) * step], expert_gate, expert_up, expert_down)
            for part in range(CHUNKS)
        ],
        axis=1,
    )
    if ONEHOT:
        weights = jnp.sum(jnp.where(hits, route_weight[:, :, None], 0.0), axis=1)
        expert_sum = jnp.dot(
            weights,
            returned.reshape(experts * capacity, -1).astype(jnp.float32),
            precision=lax.Precision.HIGHEST,
            preferred_element_type=jnp.float32,
        )
    else:
        summed = returned.astype(jnp.float32)
        results = summed.reshape(experts * capacity, -1)[target]
        expert_sum = jnp.sum(
            (results * route_weight.reshape(-1)[:, None]).reshape(row_count, TOP, -1), axis=1
        )
    return (stream.astype(jnp.float32) + expert_sum).astype(jnp.bfloat16)


def solution(mesh):
    seq_n = mesh.shape["seq"]
    exp_n = mesh.shape["exp"]
    grid = Mesh(mesh.devices.reshape(seq_n, exp_n // SPLIT, 2, SPLIT // 2), ("seq",) + EXP)
    return jax.shard_map(
        shards,
        mesh=grid,
        in_specs=(
            P("seq", EXP),
            P("seq", EXP),
            P("seq", None),
            P("seq", None),
            P(EXP, "seq"),
            P(EXP, "seq"),
            P(EXP),
            P(EXP, None),
            P(("seq",) + EXP, None),
            P(),
            P(("seq",) + EXP, None),
            P(("seq",) + EXP, None),
            P(("seq",) + EXP, None, None),
            P(("seq",) + EXP, None, None),
            P(("seq",) + EXP, None, None),
        ),
        out_specs=P(("seq",) + EXP, None),
        check_vma=False,
    )
```

```python
import jax
import jax.numpy as jnp
from jax import lax
from jax.sharding import Mesh, PartitionSpec as P

HEAD_DIM = 64
STATE = 128
TOP = 6
SPLIT = 4
STRETCH = 256
EXP = ("eh", "pz", "c")
PZ_SWAP = True
C_SWAP = True
MIX_TWO = True
MIX_SWAP = True
PREFIX_SCAN = True
CHUNKS = 1
SCAN4 = True
ONEHOT = True
CUM_DOT = True
MIX_PAIR = False


def radix_prefix(decay, state, axis):
    heads = state.shape[0]
    cut = state.shape[1] * state.shape[2]

    def join(earlier, later):
        total = earlier[:, cut] + later[:, cut]
        carried = jnp.exp(later[:, cut])[:, None] * earlier[:, :cut] + later[:, :cut]
        return jnp.concatenate([carried, jnp.broadcast_to(total[:, None], (heads, STATE))], axis=1)

    def shifted(packed, shift):
        count = lax.axis_size(axis)
        return lax.ppermute(packed, axis, perm=[(i, i + shift) for i in range(count - shift)])

    own = jnp.concatenate(
        [state.reshape(heads, cut), jnp.broadcast_to(decay[:, None], (heads, STATE))], axis=1
    )
    window = join(shifted(own, 3), join(shifted(own, 2), shifted(own, 1)))
    span = join(window, own)
    result = join(shifted(span, 12), join(shifted(span, 8), join(shifted(span, 4), window)))
    return result[:, cut], result[:, :cut].reshape(state.shape)


def expert_round(outgoing, expert_gate, expert_up, expert_down):
    arrived = lax.all_to_all(outgoing, ("seq", "eh"), split_axis=0, concat_axis=0, tiled=True)
    block = pair_gather(arrived, "pz", PZ_SWAP)
    block = pair_gather(block, "c", C_SWAP)
    flat_rows = block.reshape(-1, block.shape[-1])
    contract = (((1,), (1,)), ((), ()))
    gate_val = lax.dot_general(
        flat_rows, expert_gate[0], contract, preferred_element_type=jnp.float32
    )
    up_val = lax.dot_general(flat_rows, expert_up[0], contract, preferred_element_type=jnp.float32)
    activated = (jax.nn.silu(gate_val) * up_val).astype(jnp.bfloat16)
    piece_out = jnp.dot(activated, expert_down[0], preferred_element_type=jnp.float32).astype(
        jnp.bfloat16
    )
    piece_out = piece_out.reshape(block.shape)
    piece_sum = pair_reduce(piece_out, "c", C_SWAP)
    piece_sum = pair_reduce(piece_sum, "pz", PZ_SWAP)
    return lax.all_to_all(piece_sum, ("seq", "eh"), split_axis=0, concat_axis=0, tiled=True)


def scan_prefix(decay, state, axis):
    count = lax.axis_size(axis)
    cut = state.shape[1] * state.shape[2]
    heads = state.shape[0]

    def split(packed):
        return packed[:, cut], packed[:, :cut].reshape(state.shape)

    def join(earlier, later):
        early_decay, early_state = split(earlier)
        late_decay, late_state = split(later)
        total = early_decay + late_decay
        carried = jnp.exp(late_decay)[:, None, None] * early_state + late_state
        return jnp.concatenate(
            [carried.reshape(heads, cut), jnp.broadcast_to(total[:, None], (heads, STATE))], axis=1
        )

    packed = jnp.concatenate(
        [state.reshape(heads, cut), jnp.broadcast_to(decay[:, None], (heads, STATE))], axis=1
    )
    packed = lax.ppermute(packed, axis, perm=[(i, i + 1) for i in range(count - 1)])
    shift = 1
    while shift < count:
        moved = lax.ppermute(packed, axis, perm=[(i, i + shift) for i in range(count - shift)])
        packed = join(moved, packed)
        shift *= 2
    return split(packed)


def pair_swap(x, axis):
    return lax.ppermute(x, axis, perm=[(0, 1), (1, 0)])


def pair_gather(x, axis, swap):
    if swap:
        return jnp.stack([x, pair_swap(x, axis)])
    return lax.all_gather(x, axis)


def pair_reduce(x, axis, swap):
    if swap:
        return (x[0].astype(jnp.float32) + pair_swap(x[1], axis).astype(jnp.float32)).astype(x.dtype)
    return lax.psum_scatter(x, axis, scatter_dimension=0, tiled=True)[0]


def prefix(shard, axis, join, neutral):
    place = lax.axis_index(axis)
    decay, state = shard
    packed = jnp.concatenate(
        [state.reshape(state.shape[0], -1), jnp.broadcast_to(decay[:, None], (decay.shape[0], STATE))],
        axis=1,
    )
    gathered = lax.all_gather(packed.astype(jnp.bfloat16), axis)
    cut = state.shape[1] * state.shape[2]
    gathered = (gathered[:, :, cut], gathered[:, :, :cut].reshape((-1,) + state.shape))
    start = jax.tree.map(lambda a, e: jnp.zeros_like(a) + jnp.asarray(e, a.dtype), shard, neutral)

    def one(turn, carry):
        return join(
            carry,
            jax.tree.map(
                lambda a, own: lax.dynamic_index_in_dim(a, turn, 0, False).astype(own.dtype),
                gathered,
                shard,
            ),
        )

    return lax.fori_loop(0, place, one, start)


def join_states(earlier, later_part):
    return (
        earlier[0] + later_part[0],
        jnp.exp(later_part[0])[:, None, None] * earlier[1] + later_part[1],
    )


def shards(
    mixer_input,
    gate_input,
    write_keys,
    read_queries,
    step_size,
    log_decay,
    skip_gain,
    out_weight,
    residual,
    norm_gain,
    routes,
    route_weight,
    expert_gate,
    expert_up,
    expert_down,
):
    length = mixer_input.shape[0]
    head_count = step_size.shape[0]
    blocks = length // STRETCH
    inputs = mixer_input.reshape(blocks, STRETCH, head_count, HEAD_DIM)
    key_rows = write_keys.reshape(blocks, STRETCH, STATE)
    queries = read_queries.reshape(blocks, STRETCH, STATE)
    step_rows = step_size.reshape(head_count, blocks, STRETCH).transpose(1, 0, 2)
    if CUM_DOT:
        spots = jnp.arange(STRETCH, dtype=jnp.int32)
        upper = (spots[:, None] <= spots[None, :]).astype(jnp.float32)
        cumulative = jnp.dot(
            log_decay.reshape(head_count * blocks, STRETCH),
            upper,
            precision=lax.Precision.HIGHEST,
            preferred_element_type=jnp.float32,
        ).reshape(head_count, blocks, STRETCH).transpose(1, 0, 2)
    else:
        cumulative = jnp.cumsum(log_decay.reshape(head_count, blocks, STRETCH), axis=2).transpose(
            1, 0, 2
        )
    location_values = jnp.arange(STRETCH, dtype=jnp.int32)
    causal = location_values[:, None] >= location_values[None, :]
    scores = jnp.einsum("cin,cjn->cij", queries, key_rows, preferred_element_type=jnp.float32)
    spread = cumulative[:, :, :, None] - cumulative[:, :, None, :]
    decays = jnp.where(causal, jnp.exp(jnp.where(causal, spread, 0.0)), 0.0)
    mixing = (scores[:, None] * decays * step_rows[:, :, None, :]).astype(jnp.bfloat16)
    local_out = jnp.einsum("chij,cjhp->cihp", mixing, inputs, preferred_element_type=jnp.float32)
    tail_scale = jnp.exp(cumulative[:, :, -1:] - cumulative) * step_rows
    weighted = (inputs.astype(jnp.float32) * tail_scale.transpose(0, 2, 1)[..., None]).astype(
        jnp.bfloat16
    )
    block_state = jnp.einsum(
        "cjhp,cjn->chpn", weighted, key_rows, preferred_element_type=jnp.float32
    )
    totals = cumulative[:, :, -1]

    def advance(carry_state, pieces):
        block_total, fresh_state = pieces
        return (jnp.exp(block_total)[:, None, None] * carry_state + fresh_state, carry_state)

    zero_state = jnp.zeros((head_count, HEAD_DIM, STATE), jnp.float32)
    end_local, entering_local = lax.scan(advance, zero_state, (totals, block_state))
    device_decay = jnp.sum(totals, axis=0)
    if SCAN4 and lax.axis_size("seq") <= 16:
        before = radix_prefix(device_decay, end_local, "seq")
    elif PREFIX_SCAN:
        before = scan_prefix(device_decay, end_local, "seq")
    else:
        before = prefix(
            (device_decay, end_local), "seq", join_states, (jnp.zeros_like(device_decay), zero_state)
        )
    before_state = before[1]
    before_blocks = jnp.cumsum(totals, axis=0) - totals
    entering = jnp.exp(before_blocks)[:, :, None, None] * before_state[None] + entering_local
    carried = jnp.einsum(
        "cin,chpn->cihp", queries.astype(jnp.float32), entering, precision=lax.Precision.HIGHEST
    )
    carried = carried * jnp.exp(cumulative).transpose(0, 2, 1)[..., None]
    result = local_out + carried + skip_gain[None, None, :, None] * inputs.astype(jnp.float32)
    gated_out = (
        result.reshape(length, head_count * HEAD_DIM) * jax.nn.silu(gate_input.astype(jnp.float32))
    ).astype(jnp.bfloat16)
    row_count = residual.shape[0]
    projected = jnp.dot(gated_out, out_weight, preferred_element_type=jnp.float32).astype(
        jnp.bfloat16
    )
    if MIX_TWO:
        cores = lax.axis_size("c")
        projected = projected.reshape(-1, cores, row_count, projected.shape[-1]).transpose(1, 0, 2, 3)
        if MIX_SWAP:
            core = lax.axis_index("c")
            projected = pair_reduce(
                jnp.stack(
                    [
                        lax.dynamic_index_in_dim(projected, core, 0, False),
                        lax.dynamic_index_in_dim(projected, 1 - core, 0, False),
                    ]
                ),
                "c",
                True,
            )
        else:
            projected = lax.psum_scatter(projected, "c", scatter_dimension=0, tiled=True)[0]
        if MIX_PAIR:
            pairs = lax.axis_size("pz")
            projected = projected.reshape(-1, pairs, row_count, projected.shape[-1]).transpose(1, 0, 2, 3)
            side = lax.axis_index("pz")
            projected = pair_reduce(
                jnp.stack(
                    [
                        lax.dynamic_index_in_dim(projected, side, 0, False),
                        lax.dynamic_index_in_dim(projected, 1 - side, 0, False),
                    ]
                ),
                "pz",
                True,
            )
            mixer_out = lax.psum_scatter(projected, "eh", scatter_dimension=0, tiled=True)[0].astype(
                jnp.float32
            )
        else:
            mixer_out = lax.psum_scatter(
                projected, ("eh", "pz"), scatter_dimension=0, tiled=True
            )[0].astype(jnp.float32)
    else:
        mixer_out = lax.psum_scatter(projected, EXP, scatter_dimension=0, tiled=True).astype(
            jnp.float32
        )
    stream = (residual.astype(jnp.float32) + mixer_out).astype(jnp.bfloat16)
    widened = stream.astype(jnp.float32)
    normed = (
        widened * lax.rsqrt(jnp.mean(widened * widened, axis=-1, keepdims=True) + 1e-06) * norm_gain
    ).astype(jnp.bfloat16)
    seq_count = lax.axis_size("seq")
    exp_count = lax.axis_size(EXP)
    row_experts = exp_count // SPLIT
    experts = seq_count * row_experts
    capacity = min(row_count, max(2, (4 * TOP * row_count + 3 * experts - 1) // (3 * experts)))
    flat_routes = routes.reshape(-1)
    onehot = (flat_routes[:, None] == jnp.arange(experts, dtype=jnp.int32)[None, :]).astype(
        jnp.int32
    )
    earlier_count = jnp.cumsum(onehot, axis=0) - onehot
    slot_index = jnp.sum(earlier_count * onehot, axis=1)
    target = flat_routes * capacity + slot_index
    owner_row = jnp.arange(flat_routes.shape[0], dtype=jnp.int32) // TOP
    source = jnp.zeros((experts * capacity,), jnp.int32).at[target].set(owner_row)
    filled = jnp.zeros((experts * capacity,), jnp.bool_).at[target].set(True)
    slots = jnp.arange(experts * capacity, dtype=jnp.int32)
    hits = target.reshape(row_count, TOP)[:, :, None] == slots[None, None, :]
    if ONEHOT:
        picks = jnp.any(hits, axis=1).T.astype(jnp.bfloat16)
        outgoing = jnp.dot(picks, normed, preferred_element_type=jnp.float32).astype(jnp.bfloat16)
    else:
        outgoing = jnp.where(filled[:, None], normed[source], jnp.zeros((), jnp.bfloat16))
    outgoing = outgoing.reshape(experts, capacity, -1)
    step = capacity // CHUNKS
    returned = jnp.concatenate(
        [
            expert_round(outgoing[:, part * step : (part + 1) * step], expert_gate, expert_up, expert_down)
            for part in range(CHUNKS)
        ],
        axis=1,
    )
    if ONEHOT:
        weights = jnp.sum(jnp.where(hits, route_weight[:, :, None], 0.0), axis=1)
        expert_sum = jnp.dot(
            weights,
            returned.reshape(experts * capacity, -1).astype(jnp.float32),
            precision=lax.Precision.HIGHEST,
            preferred_element_type=jnp.float32,
        )
    else:
        summed = returned.astype(jnp.float32)
        results = summed.reshape(experts * capacity, -1)[target]
        expert_sum = jnp.sum(
            (results * route_weight.reshape(-1)[:, None]).reshape(row_count, TOP, -1), axis=1
        )
    return (stream.astype(jnp.float32) + expert_sum).astype(jnp.bfloat16)


def solution(mesh):
    seq_n = mesh.shape["seq"]
    exp_n = mesh.shape["exp"]
    grid = Mesh(mesh.devices.reshape(seq_n, exp_n // SPLIT, 2, SPLIT // 2), ("seq",) + EXP)
    return jax.shard_map(
        shards,
        mesh=grid,
        in_specs=(
            P("seq", EXP),
            P("seq", EXP),
            P("seq", None),
            P("seq", None),
            P(EXP, "seq"),
            P(EXP, "seq"),
            P(EXP),
            P(EXP, None),
            P(("seq",) + EXP, None),
            P(),
            P(("seq",) + EXP, None),
            P(("seq",) + EXP, None),
            P(("seq",) + EXP, None, None),
            P(("seq",) + EXP, None, None),
            P(("seq",) + EXP, None, None),
        ),
        out_specs=P(("seq",) + EXP, None),
        check_vma=False,
    )
```

```python
import jax
import jax.numpy as jnp
from jax import lax
from jax.sharding import Mesh, PartitionSpec as P

HEAD_DIM = 64
STATE = 128
TOP = 6
SPLIT = 4
STRETCH = 256
EXP = ("eh", "pz", "c")
PZ_SWAP = True
C_SWAP = True
MIX_TWO = True
MIX_SWAP = True
PREFIX_SCAN = True
CHUNKS = 1
SCAN4 = True
ONEHOT = True
CUM_DOT = True
MIX_PAIR = False
C_EARLY = True
UNROLL = False


def radix_prefix(decay, state, axis):
    heads = state.shape[0]
    cut = state.shape[1] * state.shape[2]

    def join(earlier, later):
        total = earlier[:, cut] + later[:, cut]
        carried = jnp.exp(later[:, cut])[:, None] * earlier[:, :cut] + later[:, :cut]
        return jnp.concatenate([carried, jnp.broadcast_to(total[:, None], (heads, STATE))], axis=1)

    def shifted(packed, shift):
        count = lax.axis_size(axis)
        return lax.ppermute(packed, axis, perm=[(i, i + shift) for i in range(count - shift)])

    own = jnp.concatenate(
        [state.reshape(heads, cut), jnp.broadcast_to(decay[:, None], (heads, STATE))], axis=1
    )
    window = join(shifted(own, 3), join(shifted(own, 2), shifted(own, 1)))
    span = join(window, own)
    result = join(shifted(span, 12), join(shifted(span, 8), join(shifted(span, 4), window)))
    return result[:, cut], result[:, :cut].reshape(state.shape)


def expert_round(outgoing, expert_gate, expert_up, expert_down):
    arrived = lax.all_to_all(outgoing, ("seq", "eh"), split_axis=0, concat_axis=0, tiled=True)
    if C_EARLY:
        partner = pair_swap(arrived, "pz")
        block = jnp.stack(
            [jnp.stack([arrived, partner]), jnp.stack([pair_swap(arrived, "c"), pair_swap(partner, "c")])]
        )
    else:
        block = pair_gather(arrived, "pz", PZ_SWAP)
        block = pair_gather(block, "c", C_SWAP)
    flat_rows = block.reshape(-1, block.shape[-1])
    contract = (((1,), (1,)), ((), ()))
    gate_val = lax.dot_general(
        flat_rows, expert_gate[0], contract, preferred_element_type=jnp.float32
    )
    up_val = lax.dot_general(flat_rows, expert_up[0], contract, preferred_element_type=jnp.float32)
    activated = (jax.nn.silu(gate_val) * up_val).astype(jnp.bfloat16)
    piece_out = jnp.dot(activated, expert_down[0], preferred_element_type=jnp.float32).astype(
        jnp.bfloat16
    )
    piece_out = piece_out.reshape(block.shape)
    piece_sum = pair_reduce(piece_out, "c", C_SWAP)
    piece_sum = pair_reduce(piece_sum, "pz", PZ_SWAP)
    return lax.all_to_all(piece_sum, ("seq", "eh"), split_axis=0, concat_axis=0, tiled=True)


def scan_prefix(decay, state, axis):
    count = lax.axis_size(axis)
    cut = state.shape[1] * state.shape[2]
    heads = state.shape[0]

    def split(packed):
        return packed[:, cut], packed[:, :cut].reshape(state.shape)

    def join(earlier, later):
        early_decay, early_state = split(earlier)
        late_decay, late_state = split(later)
        total = early_decay + late_decay
        carried = jnp.exp(late_decay)[:, None, None] * early_state + late_state
        return jnp.concatenate(
            [carried.reshape(heads, cut), jnp.broadcast_to(total[:, None], (heads, STATE))], axis=1
        )

    packed = jnp.concatenate(
        [state.reshape(heads, cut), jnp.broadcast_to(decay[:, None], (heads, STATE))], axis=1
    )
    packed = lax.ppermute(packed, axis, perm=[(i, i + 1) for i in range(count - 1)])
    shift = 1
    while shift < count:
        moved = lax.ppermute(packed, axis, perm=[(i, i + shift) for i in range(count - shift)])
        packed = join(moved, packed)
        shift *= 2
    return split(packed)


def pair_swap(x, axis):
    return lax.ppermute(x, axis, perm=[(0, 1), (1, 0)])


def pair_gather(x, axis, swap):
    if swap:
        return jnp.stack([x, pair_swap(x, axis)])
    return lax.all_gather(x, axis)


def pair_reduce(x, axis, swap):
    if swap:
        return (x[0].astype(jnp.float32) + pair_swap(x[1], axis).astype(jnp.float32)).astype(x.dtype)
    return lax.psum_scatter(x, axis, scatter_dimension=0, tiled=True)[0]


def prefix(shard, axis, join, neutral):
    place = lax.axis_index(axis)
    decay, state = shard
    packed = jnp.concatenate(
        [state.reshape(state.shape[0], -1), jnp.broadcast_to(decay[:, None], (decay.shape[0], STATE))],
        axis=1,
    )
    gathered = lax.all_gather(packed.astype(jnp.bfloat16), axis)
    cut = state.shape[1] * state.shape[2]
    gathered = (gathered[:, :, cut], gathered[:, :, :cut].reshape((-1,) + state.shape))
    start = jax.tree.map(lambda a, e: jnp.zeros_like(a) + jnp.asarray(e, a.dtype), shard, neutral)

    def one(turn, carry):
        return join(
            carry,
            jax.tree.map(
                lambda a, own: lax.dynamic_index_in_dim(a, turn, 0, False).astype(own.dtype),
                gathered,
                shard,
            ),
        )

    return lax.fori_loop(0, place, one, start)


def join_states(earlier, later_part):
    return (
        earlier[0] + later_part[0],
        jnp.exp(later_part[0])[:, None, None] * earlier[1] + later_part[1],
    )


def shards(
    mixer_input,
    gate_input,
    write_keys,
    read_queries,
    step_size,
    log_decay,
    skip_gain,
    out_weight,
    residual,
    norm_gain,
    routes,
    route_weight,
    expert_gate,
    expert_up,
    expert_down,
):
    length = mixer_input.shape[0]
    head_count = step_size.shape[0]
    blocks = length // STRETCH
    inputs = mixer_input.reshape(blocks, STRETCH, head_count, HEAD_DIM)
    key_rows = write_keys.reshape(blocks, STRETCH, STATE)
    queries = read_queries.reshape(blocks, STRETCH, STATE)
    step_rows = step_size.reshape(head_count, blocks, STRETCH).transpose(1, 0, 2)
    if CUM_DOT:
        spots = jnp.arange(STRETCH, dtype=jnp.int32)
        upper = (spots[:, None] <= spots[None, :]).astype(jnp.float32)
        cumulative = jnp.dot(
            log_decay.reshape(head_count * blocks, STRETCH),
            upper,
            precision=lax.Precision.HIGHEST,
            preferred_element_type=jnp.float32,
        ).reshape(head_count, blocks, STRETCH).transpose(1, 0, 2)
    else:
        cumulative = jnp.cumsum(log_decay.reshape(head_count, blocks, STRETCH), axis=2).transpose(
            1, 0, 2
        )
    location_values = jnp.arange(STRETCH, dtype=jnp.int32)
    causal = location_values[:, None] >= location_values[None, :]
    scores = jnp.einsum("cin,cjn->cij", queries, key_rows, preferred_element_type=jnp.float32)
    spread = cumulative[:, :, :, None] - cumulative[:, :, None, :]
    decays = jnp.where(causal, jnp.exp(jnp.where(causal, spread, 0.0)), 0.0)
    mixing = (scores[:, None] * decays * step_rows[:, :, None, :]).astype(jnp.bfloat16)
    local_out = jnp.einsum("chij,cjhp->cihp", mixing, inputs, preferred_element_type=jnp.float32)
    tail_scale = jnp.exp(cumulative[:, :, -1:] - cumulative) * step_rows
    weighted = (inputs.astype(jnp.float32) * tail_scale.transpose(0, 2, 1)[..., None]).astype(
        jnp.bfloat16
    )
    block_state = jnp.einsum(
        "cjhp,cjn->chpn", weighted, key_rows, preferred_element_type=jnp.float32
    )
    totals = cumulative[:, :, -1]

    def advance(carry_state, pieces):
        block_total, fresh_state = pieces
        return (jnp.exp(block_total)[:, None, None] * carry_state + fresh_state, carry_state)

    zero_state = jnp.zeros((head_count, HEAD_DIM, STATE), jnp.float32)
    end_local, entering_local = lax.scan(advance, zero_state, (totals, block_state), unroll=UNROLL)
    device_decay = jnp.sum(totals, axis=0)
    if SCAN4 and lax.axis_size("seq") <= 16:
        before = radix_prefix(device_decay, end_local, "seq")
    elif PREFIX_SCAN:
        before = scan_prefix(device_decay, end_local, "seq")
    else:
        before = prefix(
            (device_decay, end_local), "seq", join_states, (jnp.zeros_like(device_decay), zero_state)
        )
    before_state = before[1]
    before_blocks = jnp.cumsum(totals, axis=0) - totals
    entering = jnp.exp(before_blocks)[:, :, None, None] * before_state[None] + entering_local
    carried = jnp.einsum(
        "cin,chpn->cihp", queries.astype(jnp.float32), entering, precision=lax.Precision.HIGHEST
    )
    carried = carried * jnp.exp(cumulative).transpose(0, 2, 1)[..., None]
    result = local_out + carried + skip_gain[None, None, :, None] * inputs.astype(jnp.float32)
    gated_out = (
        result.reshape(length, head_count * HEAD_DIM) * jax.nn.silu(gate_input.astype(jnp.float32))
    ).astype(jnp.bfloat16)
    row_count = residual.shape[0]
    projected = jnp.dot(gated_out, out_weight, preferred_element_type=jnp.float32).astype(
        jnp.bfloat16
    )
    if MIX_TWO:
        cores = lax.axis_size("c")
        projected = projected.reshape(-1, cores, row_count, projected.shape[-1]).transpose(1, 0, 2, 3)
        if MIX_SWAP:
            core = lax.axis_index("c")
            projected = pair_reduce(
                jnp.stack(
                    [
                        lax.dynamic_index_in_dim(projected, core, 0, False),
                        lax.dynamic_index_in_dim(projected, 1 - core, 0, False),
                    ]
                ),
                "c",
                True,
            )
        else:
            projected = lax.psum_scatter(projected, "c", scatter_dimension=0, tiled=True)[0]
        if MIX_PAIR:
            pairs = lax.axis_size("pz")
            projected = projected.reshape(-1, pairs, row_count, projected.shape[-1]).transpose(1, 0, 2, 3)
            side = lax.axis_index("pz")
            projected = pair_reduce(
                jnp.stack(
                    [
                        lax.dynamic_index_in_dim(projected, side, 0, False),
                        lax.dynamic_index_in_dim(projected, 1 - side, 0, False),
                    ]
                ),
                "pz",
                True,
            )
            mixer_out = lax.psum_scatter(projected, "eh", scatter_dimension=0, tiled=True)[0].astype(
                jnp.float32
            )
        else:
            mixer_out = lax.psum_scatter(
                projected, ("eh", "pz"), scatter_dimension=0, tiled=True
            )[0].astype(jnp.float32)
    else:
        mixer_out = lax.psum_scatter(projected, EXP, scatter_dimension=0, tiled=True).astype(
            jnp.float32
        )
    stream = (residual.astype(jnp.float32) + mixer_out).astype(jnp.bfloat16)
    widened = stream.astype(jnp.float32)
    normed = (
        widened * lax.rsqrt(jnp.mean(widened * widened, axis=-1, keepdims=True) + 1e-06) * norm_gain
    ).astype(jnp.bfloat16)
    seq_count = lax.axis_size("seq")
    exp_count = lax.axis_size(EXP)
    row_experts = exp_count // SPLIT
    experts = seq_count * row_experts
    capacity = min(row_count, max(2, (4 * TOP * row_count + 3 * experts - 1) // (3 * experts)))
    flat_routes = routes.reshape(-1)
    onehot = (flat_routes[:, None] == jnp.arange(experts, dtype=jnp.int32)[None, :]).astype(
        jnp.int32
    )
    earlier_count = jnp.cumsum(onehot, axis=0) - onehot
    slot_index = jnp.sum(earlier_count * onehot, axis=1)
    target = flat_routes * capacity + slot_index
    owner_row = jnp.arange(flat_routes.shape[0], dtype=jnp.int32) // TOP
    source = jnp.zeros((experts * capacity,), jnp.int32).at[target].set(owner_row)
    filled = jnp.zeros((experts * capacity,), jnp.bool_).at[target].set(True)
    slots = jnp.arange(experts * capacity, dtype=jnp.int32)
    hits = target.reshape(row_count, TOP)[:, :, None] == slots[None, None, :]
    if ONEHOT:
        picks = jnp.any(hits, axis=1).T.astype(jnp.bfloat16)
        outgoing = jnp.dot(picks, normed, preferred_element_type=jnp.float32).astype(jnp.bfloat16)
    else:
        outgoing = jnp.where(filled[:, None], normed[source], jnp.zeros((), jnp.bfloat16))
    outgoing = outgoing.reshape(experts, capacity, -1)
    step = capacity // CHUNKS
    returned = jnp.concatenate(
        [
            expert_round(outgoing[:, part * step : (part + 1) * step], expert_gate, expert_up, expert_down)
            for part in range(CHUNKS)
        ],
        axis=1,
    )
    if ONEHOT:
        weights = jnp.sum(jnp.where(hits, route_weight[:, :, None], 0.0), axis=1)
        expert_sum = jnp.dot(
            weights,
            returned.reshape(experts * capacity, -1).astype(jnp.float32),
            precision=lax.Precision.HIGHEST,
            preferred_element_type=jnp.float32,
        )
    else:
        summed = returned.astype(jnp.float32)
        results = summed.reshape(experts * capacity, -1)[target]
        expert_sum = jnp.sum(
            (results * route_weight.reshape(-1)[:, None]).reshape(row_count, TOP, -1), axis=1
        )
    return (stream.astype(jnp.float32) + expert_sum).astype(jnp.bfloat16)


def solution(mesh):
    seq_n = mesh.shape["seq"]
    exp_n = mesh.shape["exp"]
    grid = Mesh(mesh.devices.reshape(seq_n, exp_n // SPLIT, 2, SPLIT // 2), ("seq",) + EXP)
    return jax.shard_map(
        shards,
        mesh=grid,
        in_specs=(
            P("seq", EXP),
            P("seq", EXP),
            P("seq", None),
            P("seq", None),
            P(EXP, "seq"),
            P(EXP, "seq"),
            P(EXP),
            P(EXP, None),
            P(("seq",) + EXP, None),
            P(),
            P(("seq",) + EXP, None),
            P(("seq",) + EXP, None),
            P(("seq",) + EXP, None, None),
            P(("seq",) + EXP, None, None),
            P(("seq",) + EXP, None, None),
        ),
        out_specs=P(("seq",) + EXP, None),
        check_vma=False,
    )
```

```python
import jax
import jax.numpy as jnp
from jax import lax
from jax.sharding import Mesh, PartitionSpec as P

HEAD_DIM = 64
STATE = 128
TOP = 6
SPLIT = 4
STRETCH = 256
EXP = ("eh", "pz", "c")
PZ_SWAP = True
C_SWAP = True
MIX_TWO = True
MIX_SWAP = True
PREFIX_SCAN = True
CHUNKS = 1
SCAN4 = True
ONEHOT = True
CUM_DOT = True
MIX_PAIR = False
C_EARLY = True
R_EARLY = True
UNROLL = False


def radix_prefix(decay, state, axis):
    heads = state.shape[0]
    cut = state.shape[1] * state.shape[2]

    def join(earlier, later):
        total = earlier[:, cut] + later[:, cut]
        carried = jnp.exp(later[:, cut])[:, None] * earlier[:, :cut] + later[:, :cut]
        return jnp.concatenate([carried, jnp.broadcast_to(total[:, None], (heads, STATE))], axis=1)

    def shifted(packed, shift):
        count = lax.axis_size(axis)
        return lax.ppermute(packed, axis, perm=[(i, i + shift) for i in range(count - shift)])

    own = jnp.concatenate(
        [state.reshape(heads, cut), jnp.broadcast_to(decay[:, None], (heads, STATE))], axis=1
    )
    window = join(shifted(own, 3), join(shifted(own, 2), shifted(own, 1)))
    span = join(window, own)
    result = join(shifted(span, 12), join(shifted(span, 8), join(shifted(span, 4), window)))
    return result[:, cut], result[:, :cut].reshape(state.shape)


def expert_round(outgoing, expert_gate, expert_up, expert_down):
    arrived = lax.all_to_all(outgoing, ("seq", "eh"), split_axis=0, concat_axis=0, tiled=True)
    if C_EARLY:
        partner = pair_swap(arrived, "pz")
        block = jnp.stack(
            [jnp.stack([arrived, partner]), jnp.stack([pair_swap(arrived, "c"), pair_swap(partner, "c")])]
        )
    else:
        block = pair_gather(arrived, "pz", PZ_SWAP)
        block = pair_gather(block, "c", C_SWAP)
    flat_rows = block.reshape(-1, block.shape[-1])
    contract = (((1,), (1,)), ((), ()))
    gate_val = lax.dot_general(
        flat_rows, expert_gate[0], contract, preferred_element_type=jnp.float32
    )
    up_val = lax.dot_general(flat_rows, expert_up[0], contract, preferred_element_type=jnp.float32)
    activated = (jax.nn.silu(gate_val) * up_val).astype(jnp.bfloat16)
    piece_out = jnp.dot(activated, expert_down[0], preferred_element_type=jnp.float32).astype(
        jnp.bfloat16
    )
    piece_out = piece_out.reshape(block.shape)
    if R_EARLY:
        crossing = pair_reduce(piece_out[:, 1], "c", True)
        arriving = pair_swap(crossing, "pz")
        staying = pair_reduce(piece_out[:, 0], "c", True)
        piece_sum = (staying.astype(jnp.float32) + arriving.astype(jnp.float32)).astype(jnp.bfloat16)
    else:
        piece_sum = pair_reduce(piece_out, "c", C_SWAP)
        piece_sum = pair_reduce(piece_sum, "pz", PZ_SWAP)
    return lax.all_to_all(piece_sum, ("seq", "eh"), split_axis=0, concat_axis=0, tiled=True)


def scan_prefix(decay, state, axis):
    count = lax.axis_size(axis)
    cut = state.shape[1] * state.shape[2]
    heads = state.shape[0]

    def split(packed):
        return packed[:, cut], packed[:, :cut].reshape(state.shape)

    def join(earlier, later):
        early_decay, early_state = split(earlier)
        late_decay, late_state = split(later)
        total = early_decay + late_decay
        carried = jnp.exp(late_decay)[:, None, None] * early_state + late_state
        return jnp.concatenate(
            [carried.reshape(heads, cut), jnp.broadcast_to(total[:, None], (heads, STATE))], axis=1
        )

    packed = jnp.concatenate(
        [state.reshape(heads, cut), jnp.broadcast_to(decay[:, None], (heads, STATE))], axis=1
    )
    packed = lax.ppermute(packed, axis, perm=[(i, i + 1) for i in range(count - 1)])
    shift = 1
    while shift < count:
        moved = lax.ppermute(packed, axis, perm=[(i, i + shift) for i in range(count - shift)])
        packed = join(moved, packed)
        shift *= 2
    return split(packed)


def pair_swap(x, axis):
    return lax.ppermute(x, axis, perm=[(0, 1), (1, 0)])


def pair_gather(x, axis, swap):
    if swap:
        return jnp.stack([x, pair_swap(x, axis)])
    return lax.all_gather(x, axis)


def pair_reduce(x, axis, swap):
    if swap:
        return (x[0].astype(jnp.float32) + pair_swap(x[1], axis).astype(jnp.float32)).astype(x.dtype)
    return lax.psum_scatter(x, axis, scatter_dimension=0, tiled=True)[0]


def prefix(shard, axis, join, neutral):
    place = lax.axis_index(axis)
    decay, state = shard
    packed = jnp.concatenate(
        [state.reshape(state.shape[0], -1), jnp.broadcast_to(decay[:, None], (decay.shape[0], STATE))],
        axis=1,
    )
    gathered = lax.all_gather(packed.astype(jnp.bfloat16), axis)
    cut = state.shape[1] * state.shape[2]
    gathered = (gathered[:, :, cut], gathered[:, :, :cut].reshape((-1,) + state.shape))
    start = jax.tree.map(lambda a, e: jnp.zeros_like(a) + jnp.asarray(e, a.dtype), shard, neutral)

    def one(turn, carry):
        return join(
            carry,
            jax.tree.map(
                lambda a, own: lax.dynamic_index_in_dim(a, turn, 0, False).astype(own.dtype),
                gathered,
                shard,
            ),
        )

    return lax.fori_loop(0, place, one, start)


def join_states(earlier, later_part):
    return (
        earlier[0] + later_part[0],
        jnp.exp(later_part[0])[:, None, None] * earlier[1] + later_part[1],
    )


def shards(
    mixer_input,
    gate_input,
    write_keys,
    read_queries,
    step_size,
    log_decay,
    skip_gain,
    out_weight,
    residual,
    norm_gain,
    routes,
    route_weight,
    expert_gate,
    expert_up,
    expert_down,
):
    length = mixer_input.shape[0]
    head_count = step_size.shape[0]
    blocks = length // STRETCH
    inputs = mixer_input.reshape(blocks, STRETCH, head_count, HEAD_DIM)
    key_rows = write_keys.reshape(blocks, STRETCH, STATE)
    queries = read_queries.reshape(blocks, STRETCH, STATE)
    step_rows = step_size.reshape(head_count, blocks, STRETCH).transpose(1, 0, 2)
    if CUM_DOT:
        spots = jnp.arange(STRETCH, dtype=jnp.int32)
        upper = (spots[:, None] <= spots[None, :]).astype(jnp.float32)
        cumulative = jnp.dot(
            log_decay.reshape(head_count * blocks, STRETCH),
            upper,
            precision=lax.Precision.HIGHEST,
            preferred_element_type=jnp.float32,
        ).reshape(head_count, blocks, STRETCH).transpose(1, 0, 2)
    else:
        cumulative = jnp.cumsum(log_decay.reshape(head_count, blocks, STRETCH), axis=2).transpose(
            1, 0, 2
        )
    location_values = jnp.arange(STRETCH, dtype=jnp.int32)
    causal = location_values[:, None] >= location_values[None, :]
    scores = jnp.einsum("cin,cjn->cij", queries, key_rows, preferred_element_type=jnp.float32)
    spread = cumulative[:, :, :, None] - cumulative[:, :, None, :]
    decays = jnp.where(causal, jnp.exp(jnp.where(causal, spread, 0.0)), 0.0)
    mixing = (scores[:, None] * decays * step_rows[:, :, None, :]).astype(jnp.bfloat16)
    local_out = jnp.einsum("chij,cjhp->cihp", mixing, inputs, preferred_element_type=jnp.float32)
    tail_scale = jnp.exp(cumulative[:, :, -1:] - cumulative) * step_rows
    weighted = (inputs.astype(jnp.float32) * tail_scale.transpose(0, 2, 1)[..., None]).astype(
        jnp.bfloat16
    )
    block_state = jnp.einsum(
        "cjhp,cjn->chpn", weighted, key_rows, preferred_element_type=jnp.float32
    )
    totals = cumulative[:, :, -1]

    def advance(carry_state, pieces):
        block_total, fresh_state = pieces
        return (jnp.exp(block_total)[:, None, None] * carry_state + fresh_state, carry_state)

    zero_state = jnp.zeros((head_count, HEAD_DIM, STATE), jnp.float32)
    end_local, entering_local = lax.scan(advance, zero_state, (totals, block_state), unroll=UNROLL)
    device_decay = jnp.sum(totals, axis=0)
    if SCAN4 and lax.axis_size("seq") <= 16:
        before = radix_prefix(device_decay, end_local, "seq")
    elif PREFIX_SCAN:
        before = scan_prefix(device_decay, end_local, "seq")
    else:
        before = prefix(
            (device_decay, end_local), "seq", join_states, (jnp.zeros_like(device_decay), zero_state)
        )
    before_state = before[1]
    before_blocks = jnp.cumsum(totals, axis=0) - totals
    entering = jnp.exp(before_blocks)[:, :, None, None] * before_state[None] + entering_local
    carried = jnp.einsum(
        "cin,chpn->cihp", queries.astype(jnp.float32), entering, precision=lax.Precision.HIGHEST
    )
    carried = carried * jnp.exp(cumulative).transpose(0, 2, 1)[..., None]
    result = local_out + carried + skip_gain[None, None, :, None] * inputs.astype(jnp.float32)
    gated_out = (
        result.reshape(length, head_count * HEAD_DIM) * jax.nn.silu(gate_input.astype(jnp.float32))
    ).astype(jnp.bfloat16)
    row_count = residual.shape[0]
    projected = jnp.dot(gated_out, out_weight, preferred_element_type=jnp.float32).astype(
        jnp.bfloat16
    )
    if MIX_TWO:
        cores = lax.axis_size("c")
        projected = projected.reshape(-1, cores, row_count, projected.shape[-1]).transpose(1, 0, 2, 3)
        if MIX_SWAP:
            core = lax.axis_index("c")
            projected = pair_reduce(
                jnp.stack(
                    [
                        lax.dynamic_index_in_dim(projected, core, 0, False),
                        lax.dynamic_index_in_dim(projected, 1 - core, 0, False),
                    ]
                ),
                "c",
                True,
            )
        else:
            projected = lax.psum_scatter(projected, "c", scatter_dimension=0, tiled=True)[0]
        if MIX_PAIR:
            pairs = lax.axis_size("pz")
            projected = projected.reshape(-1, pairs, row_count, projected.shape[-1]).transpose(1, 0, 2, 3)
            side = lax.axis_index("pz")
            projected = pair_reduce(
                jnp.stack(
                    [
                        lax.dynamic_index_in_dim(projected, side, 0, False),
                        lax.dynamic_index_in_dim(projected, 1 - side, 0, False),
                    ]
                ),
                "pz",
                True,
            )
            mixer_out = lax.psum_scatter(projected, "eh", scatter_dimension=0, tiled=True)[0].astype(
                jnp.float32
            )
        else:
            mixer_out = lax.psum_scatter(
                projected, ("eh", "pz"), scatter_dimension=0, tiled=True
            )[0].astype(jnp.float32)
    else:
        mixer_out = lax.psum_scatter(projected, EXP, scatter_dimension=0, tiled=True).astype(
            jnp.float32
        )
    stream = (residual.astype(jnp.float32) + mixer_out).astype(jnp.bfloat16)
    widened = stream.astype(jnp.float32)
    normed = (
        widened * lax.rsqrt(jnp.mean(widened * widened, axis=-1, keepdims=True) + 1e-06) * norm_gain
    ).astype(jnp.bfloat16)
    seq_count = lax.axis_size("seq")
    exp_count = lax.axis_size(EXP)
    row_experts = exp_count // SPLIT
    experts = seq_count * row_experts
    capacity = min(row_count, max(2, (4 * TOP * row_count + 3 * experts - 1) // (3 * experts)))
    flat_routes = routes.reshape(-1)
    onehot = (flat_routes[:, None] == jnp.arange(experts, dtype=jnp.int32)[None, :]).astype(
        jnp.int32
    )
    earlier_count = jnp.cumsum(onehot, axis=0) - onehot
    slot_index = jnp.sum(earlier_count * onehot, axis=1)
    target = flat_routes * capacity + slot_index
    owner_row = jnp.arange(flat_routes.shape[0], dtype=jnp.int32) // TOP
    source = jnp.zeros((experts * capacity,), jnp.int32).at[target].set(owner_row)
    filled = jnp.zeros((experts * capacity,), jnp.bool_).at[target].set(True)
    slots = jnp.arange(experts * capacity, dtype=jnp.int32)
    hits = target.reshape(row_count, TOP)[:, :, None] == slots[None, None, :]
    if ONEHOT:
        picks = jnp.any(hits, axis=1).T.astype(jnp.bfloat16)
        outgoing = jnp.dot(picks, normed, preferred_element_type=jnp.float32).astype(jnp.bfloat16)
    else:
        outgoing = jnp.where(filled[:, None], normed[source], jnp.zeros((), jnp.bfloat16))
    outgoing = outgoing.reshape(experts, capacity, -1)
    step = capacity // CHUNKS
    returned = jnp.concatenate(
        [
            expert_round(outgoing[:, part * step : (part + 1) * step], expert_gate, expert_up, expert_down)
            for part in range(CHUNKS)
        ],
        axis=1,
    )
    if ONEHOT:
        weights = jnp.sum(jnp.where(hits, route_weight[:, :, None], 0.0), axis=1)
        expert_sum = jnp.dot(
            weights,
            returned.reshape(experts * capacity, -1).astype(jnp.float32),
            precision=lax.Precision.HIGHEST,
            preferred_element_type=jnp.float32,
        )
    else:
        summed = returned.astype(jnp.float32)
        results = summed.reshape(experts * capacity, -1)[target]
        expert_sum = jnp.sum(
            (results * route_weight.reshape(-1)[:, None]).reshape(row_count, TOP, -1), axis=1
        )
    return (stream.astype(jnp.float32) + expert_sum).astype(jnp.bfloat16)


def solution(mesh):
    seq_n = mesh.shape["seq"]
    exp_n = mesh.shape["exp"]
    grid = Mesh(mesh.devices.reshape(seq_n, exp_n // SPLIT, 2, SPLIT // 2), ("seq",) + EXP)
    return jax.shard_map(
        shards,
        mesh=grid,
        in_specs=(
            P("seq", EXP),
            P("seq", EXP),
            P("seq", None),
            P("seq", None),
            P(EXP, "seq"),
            P(EXP, "seq"),
            P(EXP),
            P(EXP, None),
            P(("seq",) + EXP, None),
            P(),
            P(("seq",) + EXP, None),
            P(("seq",) + EXP, None),
            P(("seq",) + EXP, None, None),
            P(("seq",) + EXP, None, None),
            P(("seq",) + EXP, None, None),
        ),
        out_specs=P(("seq",) + EXP, None),
        check_vma=False,
    )
```
